512 devices in a mesh: slab: 16 (over y, core), gen: 32 (over z, x).
Axes of the slice: x: 4, y: 8, z: 8, core: 2. Of those that a mesh axis runs over, the one named last changes fastest.
Arguments:
- center: float32 [64, 4096], P('slab'), may hold values from -24 to 24
- generators: float32 [512, 64, 4096], P('gen', 'slab'), may hold values from -0.3 to 0.3
- conductivity: int32 [64, 4096], P('slab'), may hold values from 0 to 7
- cond_table: float32 [8], replicated, may hold values from 0.1 to 1
- direction_bank: float32 [32, 64, 4096], P(None, 'slab'), may hold values from -0.01171875 to 0.01171875
- selection: int32 [128], replicated, may hold values from 0 to 31
Outputs:
- hull_lo: float32 [64, 4096], P('slab', 'gen')
- hull_hi: float32 [64, 4096], P('slab', 'gen')
- supports: float32 [128], replicated
The draws below stay inside these ranges and needn't reach their ends.
All inputs are finite; a program needn't handle non-finite values.
Results may differ from the reference program's by a relative error of at most 0.00014.
Values sent between devices are 32-bit elements; how exact they have to be, the bound alone decides.
No kernel may reach another device: no remote copies, remote signals or barrier semaphores. Data moves between devices by JAX's collectives and lax.ppermute only.
A program may use at most 64 MiB of HBM per device.

```python
import math
import jax
import jax.numpy as jnp
from jax import lax

NX = 64
NY = 64
CLASSES = 8
BANK = 32
NDIR = 128
NZ = 64
GENS = 512
N_GEN = 32


def place_ends(values, own_key, smallest, high):
    longest = values.shape.index(max(values.shape))
    spots = []
    for shift in (0, 1):
        where = [jax.random.randint(jax.random.fold_in(own_key, axis), (), 0, length) for axis, length in enumerate(values.shape)]
        where[longest] = (where[longest] + shift) % values.shape[longest]
        spots.append(tuple(where))
    return values.at[spots[0]].set(smallest).at[spots[1]].set(high)


def strengthened(values, stream_key, source, target, blocks, factor):
    owner, partner = [(jnp.arange(values.shape[axis_at]) // (values.shape[axis_at] // blocks)).reshape([-1 if axis == axis_at else 1 for axis in range(values.ndim)]) for axis_at in (source, target)]
    chosen = jax.random.permutation(stream_key, blocks)[partner]
    strong = (owner == chosen) | (owner == (partner + blocks // 2) % blocks)
    return jnp.where(strong, factor * values, values)


def shard_levels(own_key, shape, split, low, largest):
    def one(axis_at, parts):
        steps = jax.random.uniform(jax.random.fold_in(jax.random.fold_in(own_key, 6), axis_at), (parts,), jnp.float32, low / len(split), largest / len(split))
        return jnp.repeat(jnp.exp(steps), shape[axis_at] // parts).reshape((-1,) + (1,) * (len(shape) - axis_at - 1))

    gain = one(*split[0])
    for cut in split[1:]:
        gain = gain * one(*cut)
    return gain


def scatter_about(key, extent, deviation, reach, shards=(), kind=jnp.bfloat16):
    result = jax.random.normal(key, extent, jnp.float32) * deviation
    if len(shards) > 0:
        result = shard_levels(key, extent, shards, -0.22, 0.18) * result
    return jnp.clip(result, min=-reach, max=reach).astype(kind)


def heavy_noise(key, dims, spread, reach, cuts, heavy, kind=jnp.bfloat16):
    result = spread * jax.random.normal(key, dims, jnp.float32)
    if cuts:
        result = result * shard_levels(key, dims, cuts, -0.22, 0.18)
    return jnp.clip(strengthened(result, jax.random.fold_in(key, 3), *heavy), -reach, reach).astype(kind)


def setup_inputs(seed: int = 0) -> dict:
    streams_of = jax.random.split(jax.random.key(seed), 7)
    return {
        "center": scatter_about(streams_of[0], (NZ, NX * NY), 4.0, 24.0, ((0, 16),), jnp.float32),
        "generators": heavy_noise(streams_of[1], (GENS, NZ, NX * NY), 0.05, 0.3, ((0, 32), (1, 16)), (0, 2, 32, 2.75), jnp.float32),
        "conductivity": place_ends(jax.random.randint(streams_of[2], (NZ, NX * NY), 0, CLASSES), jax.random.fold_in(streams_of[2], 1), 0, CLASSES - 1).astype(jnp.int32),
        "cond_table": jnp.clip(jnp.exp(jax.random.uniform(streams_of[3], (CLASSES,), jnp.float32, math.log(0.1), math.log(1.0))), 0.1, 1.0),
        "direction_bank": scatter_about(streams_of[4], (BANK, NZ, NX * NY), (NZ * NX * NY) ** -0.5, 0.01171875, ((1, 16),), jnp.float32),
        "selection": place_ends(jax.random.randint(streams_of[5], (NDIR,), 0, BANK), jax.random.fold_in(streams_of[5], 1), 0, BANK - 1).astype(jnp.int32),
    }


TIME_STEP = 0.16


def lookup_rate(conductivity, cond_table):
    classes = jnp.arange(cond_table.shape[0], dtype=jnp.int32)
    picked = jnp.where(conductivity[None] == classes[:, None, None], cond_table[:, None, None], jnp.float32(0.0))
    return TIME_STEP * jnp.sum(picked, axis=0)


def lateral(middle):
    cells = NX * NY
    column = jnp.arange(cells, dtype=jnp.int32) % NY
    widths = [(0, 0)] * (middle.ndim - 1) + [(NY, NY)]
    padded = jnp.pad(middle, widths)
    total = padded[..., 2 * NY:] + padded[..., :cells]
    plus = jnp.where(column < NY - 1, padded[..., NY + 1:NY + 1 + cells], jnp.float32(0.0))
    minus = jnp.where(column > 0, padded[..., NY - 1:NY - 1 + cells], jnp.float32(0.0))
    return total + plus + minus


def update(extended, rate_field):
    middle = extended[:, 1:-1]
    zsum = extended[:, 2:] + extended[:, :-2]
    return middle + rate_field * (zsum + lateral(middle) - 6.0 * middle)


def advance(fields, rate_field):
    for turn in range(2):
        fields = update(jnp.pad(fields, ((0, 0), (1, 1), (0, 0))), rate_field)
    return fields


def reference(center, generators, conductivity, cond_table, direction_bank, selection):
    rate_field = lookup_rate(conductivity, cond_table)
    centre_moved = advance(center[None], rate_field)[0]
    blocks = generators.reshape(N_GEN, GENS // N_GEN, NZ, NX * NY)

    def accumulate(carry, block):
        radius, magnitude = carry
        moved = advance(block, rate_field)
        radius = radius + jnp.sum(jnp.abs(moved), axis=0)
        proj = jnp.einsum('bzc,gzc->bg', direction_bank, moved, precision=lax.Precision.HIGHEST)
        magnitude = magnitude + jnp.sum(jnp.abs(proj), axis=1)
        return (radius, magnitude), None

    start = (jnp.zeros((NZ, NX * NY), jnp.float32), jnp.zeros((BANK,), jnp.float32))
    (radius, magnitude), unused = lax.scan(accumulate, start, blocks)
    cproj = jnp.einsum('bzc,zc->b', direction_bank, centre_moved, precision=lax.Precision.HIGHEST)
    bank_support = cproj + magnitude
    supports = bank_support[selection]
    return centre_moved - radius, centre_moved + radius, supports
```

```python
import jax
import jax.numpy as jnp
from jax import lax
from jax.sharding import PartitionSpec as P

NX = 64
NY = 64


TIME_STEP = 0.16


def padded_2(x, sides, width):
    for axis, dim in sides:
        size, length = (lax.axis_size(axis), x.shape[dim])
        up = [(i, (i + 1) % size) for i in range(size - 1)]
        down = [(j, i) for i, j in up]
        last = lax.slice_in_dim(x, length - width, length, axis=dim)
        leading = lax.slice_in_dim(x, 0, width, axis=dim)
        before = lax.ppermute(last, axis, up)
        after = lax.ppermute(leading, axis, down)
        x = jnp.concatenate([before, x, after], axis=dim)
    return x


def lookup_rate(conductivity, cond_table):
    classes = jnp.arange(cond_table.shape[0], dtype=jnp.int32)
    picked = jnp.where(
        conductivity[None] == classes[:, None, None], cond_table[:, None, None], jnp.float32(0.0)
    )
    return TIME_STEP * jnp.sum(picked, axis=0)


def lateral(middle):
    cells = NX * NY
    column = jnp.arange(cells, dtype=jnp.int32) % NY
    widths = [(0, 0)] * (middle.ndim - 1) + [(NY, NY)]
    padded = jnp.pad(middle, widths)
    total = padded[..., 2 * NY :] + padded[..., :cells]
    plus = jnp.where(column < NY - 1, padded[..., NY + 1 : NY + 1 + cells], jnp.float32(0.0))
    minus = jnp.where(column > 0, padded[..., NY - 1 : NY - 1 + cells], jnp.float32(0.0))
    return total + plus + minus


def update(extended, rate_field):
    middle = extended[:, 1:-1]
    zsum = extended[:, 2:] + extended[:, :-2]
    return middle + rate_field * (zsum + lateral(middle) - 6.0 * middle)


def select_rows(selection, values):
    entries = jnp.arange(values.shape[0], dtype=jnp.int32)
    return jnp.sum(
        jnp.where(selection[:, None] == entries[None, :], values[None, :], jnp.float32(0.0)), axis=1
    )


def butterfly_sum(x, axis):
    size = lax.axis_size(axis)
    bit = 1
    while bit < size:
        pairs = [(i, i ^ bit) for i in range(size)]
        x = x + lax.ppermute(x, axis, pairs)
        bit *= 2
    return x


def butterfly_scatter(x, axis):
    size = lax.axis_size(axis)
    me = lax.axis_index(axis)
    bit = size // 2
    while bit >= 1:
        half = x.shape[1] // 2
        lo, hi = x[:, :half], x[:, half:]
        upper = (me // bit) % 2 == 1
        keep = jnp.where(upper, hi, lo)
        send = jnp.where(upper, lo, hi)
        pairs = [(i, i ^ bit) for i in range(size)]
        x = keep + lax.ppermute(send, axis, pairs)
        bit //= 2
    return x


def per_device(center, generators, conductivity, cond_table, direction_bank, selection):
    rate_field = lookup_rate(conductivity, cond_table)
    fields = jnp.concatenate([center[None], generators], axis=0)
    for turn in range(2):
        extended = padded_2(fields, (("slab", 1),), 1)
        fields = update(extended, rate_field)
    centre_moved = fields[0]
    gens_moved = fields[1:]
    radius_local = jnp.sum(jnp.abs(gens_moved), axis=0)
    radius = butterfly_scatter(radius_local, "gen")
    columns = radius.shape[1]
    centre_cols = lax.dynamic_slice_in_dim(
        centre_moved, lax.axis_index("gen") * columns, columns, 1
    )
    hull_lo = centre_cols - radius
    hull_hi = centre_cols + radius
    bank_proj = jnp.einsum(
        "bzc,gzc->bg", direction_bank, gens_moved, precision=lax.Precision.HIGHEST
    )
    centre_proj = jnp.einsum(
        "bzc,zc->b", direction_bank, centre_moved, precision=lax.Precision.HIGHEST
    )
    both = butterfly_sum(jnp.concatenate([bank_proj, centre_proj[:, None]], axis=1), "slab")
    summed_proj, summed_centre = both[:, :-1], both[:, -1]
    partial_value = jnp.sum(jnp.abs(summed_proj), axis=1)
    magnitude = butterfly_sum(partial_value, "gen")
    bank_support = summed_centre + magnitude
    supports = select_rows(selection, bank_support)
    return (hull_lo, hull_hi, supports)


def solution(mesh):
    in_specs = (
        P("slab", None),
        P("gen", "slab", None),
        P("slab", None),
        P(),
        P(None, "slab", None),
        P(),
    )
    out_specs = (P("slab", "gen"), P("slab", "gen"), P())
    return jax.shard_map(
        per_device, mesh=mesh, in_specs=in_specs, out_specs=out_specs, check_vma=False
    )
```

```python
import jax
import jax.numpy as jnp
from jax import lax
from jax.sharding import PartitionSpec as P

NX = 64
NY = 64


TIME_STEP = 0.16


def padded_2(x, sides, width):
    for axis, dim in sides:
        size, length = (lax.axis_size(axis), x.shape[dim])
        up = [(i, (i + 1) % size) for i in range(size - 1)]
        down = [(j, i) for i, j in up]
        last = lax.slice_in_dim(x, length - width, length, axis=dim)
        leading = lax.slice_in_dim(x, 0, width, axis=dim)
        before = lax.ppermute(last, axis, up)
        after = lax.ppermute(leading, axis, down)
        x = jnp.concatenate([before, x, after], axis=dim)
    return x


def lookup_rate(conductivity, cond_table):
    classes = jnp.arange(cond_table.shape[0], dtype=jnp.int32)
    picked = jnp.where(
        conductivity[None] == classes[:, None, None], cond_table[:, None, None], jnp.float32(0.0)
    )
    return TIME_STEP * jnp.sum(picked, axis=0)


def lateral(middle):
    cells = NX * NY
    column = jnp.arange(cells, dtype=jnp.int32) % NY
    widths = [(0, 0)] * (middle.ndim - 1) + [(NY, NY)]
    padded = jnp.pad(middle, widths)
    total = padded[..., 2 * NY :] + padded[..., :cells]
    plus = jnp.where(column < NY - 1, padded[..., NY + 1 : NY + 1 + cells], jnp.float32(0.0))
    minus = jnp.where(column > 0, padded[..., NY - 1 : NY - 1 + cells], jnp.float32(0.0))
    return total + plus + minus


def update(extended, rate_field):
    middle = extended[:, 1:-1]
    zsum = extended[:, 2:] + extended[:, :-2]
    return middle + rate_field * (zsum + lateral(middle) - 6.0 * middle)


def select_rows(selection, values):
    entries = jnp.arange(values.shape[0], dtype=jnp.int32)
    return jnp.sum(
        jnp.where(selection[:, None] == entries[None, :], values[None, :], jnp.float32(0.0)), axis=1
    )


def butterfly_sum(x, axis):
    size = lax.axis_size(axis)
    bit = 1
    while bit < size:
        pairs = [(i, i ^ bit) for i in range(size)]
        x = x + lax.ppermute(x, axis, pairs)
        bit *= 2
    return x


def butterfly_scatter(x, extra, axis):
    size = lax.axis_size(axis)
    me = lax.axis_index(axis)
    bit = size // 2
    while bit >= 1:
        half = x.shape[1] // 2
        lo, hi = x[:, :half], x[:, half:]
        upper = (me // bit) % 2 == 1
        keep = jnp.where(upper, hi, lo)
        send = jnp.where(upper, lo, hi)
        pairs = [(i, i ^ bit) for i in range(size)]
        message = jnp.concatenate([send.reshape(-1), extra])
        got = lax.ppermute(message, axis, pairs)
        x = keep + got[: send.size].reshape(send.shape)
        extra = extra + got[send.size :]
        bit //= 2
    return x, extra


def per_device(center, generators, conductivity, cond_table, direction_bank, selection):
    rate_field = lookup_rate(conductivity, cond_table)
    packed = jnp.concatenate([center[None], generators, rate_field[None]], axis=0)
    extended = padded_2(packed, (("slab", 1),), 2)
    fields, rate_ext = extended[:-1], extended[-1]
    fields = update(fields, rate_ext[1:-1])
    fields = update(fields, rate_field)
    centre_moved = fields[0]
    gens_moved = fields[1:]
    radius_local = jnp.sum(jnp.abs(gens_moved), axis=0)
    all_proj = jnp.einsum(
        "bzc,gzc->bg", direction_bank, fields, precision=lax.Precision.HIGHEST
    )
    summed = butterfly_sum(all_proj, "slab")
    summed_centre, summed_proj = summed[:, 0], summed[:, 1:]
    partial_value = jnp.sum(jnp.abs(summed_proj), axis=1)
    radius, magnitude = butterfly_scatter(radius_local, partial_value, "gen")
    columns = radius.shape[1]
    centre_cols = lax.dynamic_slice_in_dim(
        centre_moved, lax.axis_index("gen") * columns, columns, 1
    )
    hull_lo = centre_cols - radius
    hull_hi = centre_cols + radius
    bank_support = summed_centre + magnitude
    supports = select_rows(selection, bank_support)
    return (hull_lo, hull_hi, supports)


def solution(mesh):
    in_specs = (
        P("slab", None),
        P("gen", "slab", None),
        P("slab", None),
        P(),
        P(None, "slab", None),
        P(),
    )
    out_specs = (P("slab", "gen"), P("slab", "gen"), P())
    return jax.shard_map(
        per_device, mesh=mesh, in_specs=in_specs, out_specs=out_specs, check_vma=False
    )
```

```python
import jax
import jax.numpy as jnp
from jax import lax
from jax.sharding import PartitionSpec as P

NX = 64
NY = 64


TIME_STEP = 0.16


def padded_2(x, sides, width):
    for axis, dim in sides:
        size, length = (lax.axis_size(axis), x.shape[dim])
        up = [(i, (i + 1) % size) for i in range(size - 1)]
        down = [(j, i) for i, j in up]
        last = lax.slice_in_dim(x, length - width, length, axis=dim)
        leading = lax.slice_in_dim(x, 0, width, axis=dim)
        before = lax.ppermute(last, axis, up)
        after = lax.ppermute(leading, axis, down)
        x = jnp.concatenate([before, x, after], axis=dim)
    return x


def lookup_rate(conductivity, cond_table):
    classes = jnp.arange(cond_table.shape[0], dtype=jnp.int32)
    picked = jnp.where(
        conductivity[None] == classes[:, None, None], cond_table[:, None, None], jnp.float32(0.0)
    )
    return TIME_STEP * jnp.sum(picked, axis=0)


def lateral(middle):
    cells = NX * NY
    column = jnp.arange(cells, dtype=jnp.int32) % NY
    widths = [(0, 0)] * (middle.ndim - 1) + [(NY, NY)]
    padded = jnp.pad(middle, widths)
    total = padded[..., 2 * NY :] + padded[..., :cells]
    plus = jnp.where(column < NY - 1, padded[..., NY + 1 : NY + 1 + cells], jnp.float32(0.0))
    minus = jnp.where(column > 0, padded[..., NY - 1 : NY - 1 + cells], jnp.float32(0.0))
    return total + plus + minus


def update(extended, rate_field):
    middle = extended[:, 1:-1]
    zsum = extended[:, 2:] + extended[:, :-2]
    return middle + rate_field * (zsum + lateral(middle) - 6.0 * middle)


def select_rows(selection, values):
    entries = jnp.arange(values.shape[0], dtype=jnp.int32)
    return jnp.sum(
        jnp.where(selection[:, None] == entries[None, :], values[None, :], jnp.float32(0.0)), axis=1
    )


def exchange_sum(x, axis):
    size = lax.axis_size(axis)
    copies = jnp.broadcast_to(x[None], (size,) + x.shape)
    received = lax.all_to_all(copies, axis, 0, 0, tiled=False)
    return jnp.sum(received, axis=0)


def exchange_scatter(x, extra, axis):
    size = lax.axis_size(axis)
    rows, cols = x.shape
    width = cols // size
    blocks = x.reshape(rows, size, width).transpose(1, 0, 2).reshape(size, rows * width)
    extras = jnp.broadcast_to(extra[None], (size, extra.shape[0]))
    message = jnp.concatenate([blocks, extras], axis=1)
    received = jnp.sum(lax.all_to_all(message, axis, 0, 0, tiled=True), axis=0)
    return received[: rows * width].reshape(rows, width), received[rows * width :]


def per_device(center, generators, conductivity, cond_table, direction_bank, selection):
    rate_field = lookup_rate(conductivity, cond_table)
    packed = jnp.concatenate([center[None], generators, rate_field[None]], axis=0)
    extended = padded_2(packed, (("slab", 1),), 2)
    fields, rate_ext = extended[:-1], extended[-1]
    fields = update(fields, rate_ext[1:-1])
    fields = update(fields, rate_field)
    centre_moved = fields[0]
    gens_moved = fields[1:]
    radius_local = jnp.sum(jnp.abs(gens_moved), axis=0)
    all_proj = jnp.einsum(
        "bzc,gzc->bg", direction_bank, fields, precision=lax.Precision.HIGHEST
    )
    summed = exchange_sum(all_proj, "slab")
    summed_centre, summed_proj = summed[:, 0], summed[:, 1:]
    partial_value = jnp.sum(jnp.abs(summed_proj), axis=1)
    radius, magnitude = exchange_scatter(radius_local, partial_value, "gen")
    columns = radius.shape[1]
    centre_cols = lax.dynamic_slice_in_dim(
        centre_moved, lax.axis_index("gen") * columns, columns, 1
    )
    hull_lo = centre_cols - radius
    hull_hi = centre_cols + radius
    bank_support = summed_centre + magnitude
    supports = select_rows(selection, bank_support)
    return (hull_lo, hull_hi, supports)


def solution(mesh):
    in_specs = (
        P("slab", None),
        P("gen", "slab", None),
        P("slab", None),
        P(),
        P(None, "slab", None),
        P(),
    )
    out_specs = (P("slab", "gen"), P("slab", "gen"), P())
    return jax.shard_map(
        per_device, mesh=mesh, in_specs=in_specs, out_specs=out_specs, check_vma=False
    )
```

```python
import jax
import jax.numpy as jnp
from jax import lax
from jax.sharding import PartitionSpec as P

NX = 64
NY = 64


TIME_STEP = 0.16


def padded_2(x, sides, width):
    for axis, dim in sides:
        size, length = (lax.axis_size(axis), x.shape[dim])
        up = [(i, (i + 1) % size) for i in range(size - 1)]
        down = [(j, i) for i, j in up]
        last = lax.slice_in_dim(x, length - width, length, axis=dim)
        leading = lax.slice_in_dim(x, 0, width, axis=dim)
        before = lax.ppermute(last, axis, up)
        after = lax.ppermute(leading, axis, down)
        x = jnp.concatenate([before, x, after], axis=dim)
    return x


def lookup_rate(conductivity, cond_table):
    classes = jnp.arange(cond_table.shape[0], dtype=jnp.int32)
    picked = jnp.where(
        conductivity[None] == classes[:, None, None], cond_table[:, None, None], jnp.float32(0.0)
    )
    return TIME_STEP * jnp.sum(picked, axis=0)


def lateral(middle):
    cells = NX * NY
    column = jnp.arange(cells, dtype=jnp.int32) % NY
    widths = [(0, 0)] * (middle.ndim - 1) + [(NY, NY)]
    padded = jnp.pad(middle, widths)
    total = padded[..., 2 * NY :] + padded[..., :cells]
    plus = jnp.where(column < NY - 1, padded[..., NY + 1 : NY + 1 + cells], jnp.float32(0.0))
    minus = jnp.where(column > 0, padded[..., NY - 1 : NY - 1 + cells], jnp.float32(0.0))
    return total + plus + minus


def update(extended, rate_field):
    middle = extended[:, 1:-1]
    zsum = extended[:, 2:] + extended[:, :-2]
    return middle + rate_field * (zsum + lateral(middle) - 6.0 * middle)


def select_rows(selection, values):
    entries = jnp.arange(values.shape[0], dtype=jnp.int32)
    return jnp.sum(
        jnp.where(selection[:, None] == entries[None, :], values[None, :], jnp.float32(0.0)), axis=1
    )


def exchange_sum(x, axis):
    size = lax.axis_size(axis)
    copies = jnp.broadcast_to(x[None], (size,) + x.shape)
    received = lax.all_to_all(copies, axis, 0, 0, tiled=False)
    return jnp.sum(received, axis=0)


def exchange_scatter(x, extra, axis):
    size = lax.axis_size(axis)
    rows, cols = x.shape
    width = cols // size
    blocks = x.reshape(rows, size, width).transpose(1, 0, 2).reshape(size, rows * width)
    extras = jnp.broadcast_to(extra[None], (size, extra.shape[0]))
    message = jnp.concatenate([blocks, extras], axis=1)
    received = jnp.sum(lax.all_to_all(message, axis, 0, 0, tiled=True), axis=0)
    return received[: rows * width].reshape(rows, width), received[rows * width :]


def per_device(center, generators, conductivity, cond_table, direction_bank, selection):
    rate_field = lookup_rate(conductivity, cond_table)
    body = jnp.concatenate([center[None], generators], axis=0)
    size = lax.axis_size("slab")
    up = [(i, i + 1) for i in range(size - 1)]
    down = [(j, i) for i, j in up]
    planes = body.shape[1]
    lower = jnp.concatenate([body[:, :2], rate_field[None, :2]], axis=0)
    upper = jnp.concatenate([body[:, planes - 2 :], rate_field[None, planes - 2 :]], axis=0)
    before = lax.ppermute(upper, "slab", up)
    after = lax.ppermute(lower, "slab", down)
    fields = jnp.concatenate([before[:-1], body, after[:-1]], axis=1)
    rate_ext = jnp.concatenate([before[-1, 1:], rate_field, after[-1, :1]], axis=0)
    fields = update(fields, rate_ext)
    fields = update(fields, rate_field)
    centre_moved = fields[0]
    gens_moved = fields[1:]
    radius_local = jnp.sum(jnp.abs(gens_moved), axis=0)
    all_proj = jnp.einsum(
        "bzc,gzc->bg", direction_bank, fields, precision=lax.Precision.HIGH
    )
    summed = exchange_sum(all_proj, "slab")
    summed_centre, summed_proj = summed[:, 0], summed[:, 1:]
    partial_value = jnp.sum(jnp.abs(summed_proj), axis=1)
    radius, magnitude = exchange_scatter(radius_local, partial_value, "gen")
    columns = radius.shape[1]
    centre_cols = lax.dynamic_slice_in_dim(
        centre_moved, lax.axis_index("gen") * columns, columns, 1
    )
    hull_lo = centre_cols - radius
    hull_hi = centre_cols + radius
    bank_support = summed_centre + magnitude
    supports = select_rows(selection, bank_support)
    return (hull_lo, hull_hi, supports)


def solution(mesh):
    in_specs = (
        P("slab", None),
        P("gen", "slab", None),
        P("slab", None),
        P(),
        P(None, "slab", None),
        P(),
    )
    out_specs = (P("slab", "gen"), P("slab", "gen"), P())
    return jax.shard_map(
        per_device, mesh=mesh, in_specs=in_specs, out_specs=out_specs, check_vma=False
    )
```

```python
import jax
import jax.numpy as jnp
from jax import lax
from jax.sharding import PartitionSpec as P

NX = 64
NY = 64


TIME_STEP = 0.16


def padded_2(x, sides, width):
    for axis, dim in sides:
        size, length = (lax.axis_size(axis), x.shape[dim])
        up = [(i, (i + 1) % size) for i in range(size - 1)]
        down = [(j, i) for i, j in up]
        last = lax.slice_in_dim(x, length - width, length, axis=dim)
        leading = lax.slice_in_dim(x, 0, width, axis=dim)
        before = lax.ppermute(last, axis, up)
        after = lax.ppermute(leading, axis, down)
        x = jnp.concatenate([before, x, after], axis=dim)
    return x


def lookup_rate(conductivity, cond_table):
    classes = jnp.arange(cond_table.shape[0], dtype=jnp.int32)
    picked = jnp.where(
        conductivity[None] == classes[:, None, None], cond_table[:, None, None], jnp.float32(0.0)
    )
    return TIME_STEP * jnp.sum(picked, axis=0)


def lateral(middle):
    cells = NX * NY
    column = jnp.arange(cells, dtype=jnp.int32) % NY
    widths = [(0, 0)] * (middle.ndim - 1) + [(NY, NY)]
    padded = jnp.pad(middle, widths)
    total = padded[..., 2 * NY :] + padded[..., :cells]
    plus = jnp.where(column < NY - 1, padded[..., NY + 1 : NY + 1 + cells], jnp.float32(0.0))
    minus = jnp.where(column > 0, padded[..., NY - 1 : NY - 1 + cells], jnp.float32(0.0))
    return total + plus + minus


def update(extended, rate_field):
    middle = extended[:, 1:-1]
    zsum = extended[:, 2:] + extended[:, :-2]
    return middle + rate_field * (zsum + lateral(middle) - 6.0 * middle)


def select_rows(selection, values):
    entries = jnp.arange(values.shape[0], dtype=jnp.int32)
    return jnp.sum(
        jnp.where(selection[:, None] == entries[None, :], values[None, :], jnp.float32(0.0)), axis=1
    )


def exchange_sum(x, axis):
    size = lax.axis_size(axis)
    copies = jnp.broadcast_to(x[None], (size,) + x.shape)
    received = lax.all_to_all(copies, axis, 0, 0, tiled=False)
    return jnp.sum(received, axis=0)


def exchange_scatter(x, extra, axis):
    size = lax.axis_size(axis)
    rows, cols = x.shape
    width = cols // size
    blocks = x.reshape(rows, size, width).transpose(1, 0, 2).reshape(size, rows * width)
    extras = jnp.broadcast_to(extra[None], (size, extra.shape[0]))
    message = jnp.concatenate([blocks, extras], axis=1)
    received = jnp.sum(lax.all_to_all(message, axis, 0, 0, tiled=True), axis=0)
    return received[: rows * width].reshape(rows, width), received[rows * width :]


def per_device(center, generators, conductivity, cond_table, direction_bank, selection):
    rate_field = lookup_rate(conductivity, cond_table)
    size = lax.axis_size("slab")
    up = [(i, i + 1) for i in range(size - 1)]
    down = [(j, i) for i, j in up]
    planes = center.shape[0]
    lower = jnp.concatenate(
        [center[None, :2], generators[:, :2], rate_field[None, :2]], axis=0
    )
    upper = jnp.concatenate(
        [center[None, planes - 2 :], generators[:, planes - 2 :], rate_field[None, planes - 2 :]],
        axis=0,
    )
    before = lax.ppermute(upper, "slab", up)
    after = lax.ppermute(lower, "slab", down)
    body = jnp.concatenate(lax.optimization_barrier([center[None], generators]), axis=0)
    fields = jnp.concatenate([before[:-1], body, after[:-1]], axis=1)
    rate_ext = jnp.concatenate([before[-1, 1:], rate_field, after[-1, :1]], axis=0)
    fields = update(fields, rate_ext)
    fields = update(fields, rate_field)
    centre_moved = fields[0]
    gens_moved = fields[1:]
    radius_local = jnp.sum(jnp.abs(gens_moved), axis=0)
    all_proj = jnp.einsum(
        "bzc,gzc->bg", direction_bank, fields, precision=lax.Precision.HIGH
    )
    summed = exchange_sum(all_proj, "slab")
    summed_centre, summed_proj = summed[:, 0], summed[:, 1:]
    partial_value = jnp.sum(jnp.abs(summed_proj), axis=1)
    radius, magnitude = exchange_scatter(radius_local, partial_value, "gen")
    columns = radius.shape[1]
    centre_cols = lax.dynamic_slice_in_dim(
        centre_moved, lax.axis_index("gen") * columns, columns, 1
    )
    hull_lo = centre_cols - radius
    hull_hi = centre_cols + radius
    bank_support = summed_centre + magnitude
    supports = select_rows(selection, bank_support)
    return (hull_lo, hull_hi, supports)


def solution(mesh):
    in_specs = (
        P("slab", None),
        P("gen", "slab", None),
        P("slab", None),
        P(),
        P(None, "slab", None),
        P(),
    )
    out_specs = (P("slab", "gen"), P("slab", "gen"), P())
    return jax.shard_map(
        per_device, mesh=mesh, in_specs=in_specs, out_specs=out_specs, check_vma=False
    )
```

```python
import jax
import jax.numpy as jnp
from jax import lax
from jax.sharding import PartitionSpec as P
from jax.experimental import pallas as pl
from jax.experimental.pallas import tpu as pltpu

NX = 64
NY = 64


TIME_STEP = 0.16


def padded_2(x, sides, width):
    for axis, dim in sides:
        size, length = (lax.axis_size(axis), x.shape[dim])
        up = [(i, (i + 1) % size) for i in range(size - 1)]
        down = [(j, i) for i, j in up]
        last = lax.slice_in_dim(x, length - width, length, axis=dim)
        leading = lax.slice_in_dim(x, 0, width, axis=dim)
        before = lax.ppermute(last, axis, up)
        after = lax.ppermute(leading, axis, down)
        x = jnp.concatenate([before, x, after], axis=dim)
    return x


def lookup_rate(conductivity, cond_table):
    classes = jnp.arange(cond_table.shape[0], dtype=jnp.int32)
    picked = jnp.where(
        conductivity[None] == classes[:, None, None], cond_table[:, None, None], jnp.float32(0.0)
    )
    return TIME_STEP * jnp.sum(picked, axis=0)


def lateral(middle):
    cells = NX * NY
    column = jnp.arange(cells, dtype=jnp.int32) % NY
    widths = [(0, 0)] * (middle.ndim - 1) + [(NY, NY)]
    padded = jnp.pad(middle, widths)
    total = padded[..., 2 * NY :] + padded[..., :cells]
    plus = jnp.where(column < NY - 1, padded[..., NY + 1 : NY + 1 + cells], jnp.float32(0.0))
    minus = jnp.where(column > 0, padded[..., NY - 1 : NY - 1 + cells], jnp.float32(0.0))
    return total + plus + minus


def update(extended, rate_field):
    middle = extended[:, 1:-1]
    zsum = extended[:, 2:] + extended[:, :-2]
    return middle + rate_field * (zsum + lateral(middle) - 6.0 * middle)


def select_rows(selection, values):
    entries = jnp.arange(values.shape[0], dtype=jnp.int32)
    return jnp.sum(
        jnp.where(selection[:, None] == entries[None, :], values[None, :], jnp.float32(0.0)), axis=1
    )


def exchange_sum(x, axis):
    size = lax.axis_size(axis)
    copies = jnp.broadcast_to(x[None], (size,) + x.shape)
    received = lax.all_to_all(copies, axis, 0, 0, tiled=False)
    return jnp.sum(received, axis=0)


def exchange_scatter(x, extra, axis):
    size = lax.axis_size(axis)
    rows, cols = x.shape
    width = cols // size
    blocks = x.reshape(rows, size, width).transpose(1, 0, 2).reshape(size, rows * width)
    extras = jnp.broadcast_to(extra[None], (size, extra.shape[0]))
    message = jnp.concatenate([blocks, extras], axis=1)
    received = jnp.sum(lax.all_to_all(message, axis, 0, 0, tiled=True), axis=0)
    return received[: rows * width].reshape(rows, width), received[rows * width :]


def stencil_kernel(ext_ref, rate_ref, bank_ref, centre_ref, radius_ref, prod_ref, moved_ref):
    rate = rate_ref[...]
    rows, cells = rate.shape
    lane = lax.broadcasted_iota(jnp.int32, (rows, cells), 1)
    column = lane % NY
    has_next = lane < cells - NY
    has_prev = lane >= NY
    has_plus = column < NY - 1
    has_minus = column > 0
    zero = jnp.float32(0.0)

    def step(u):
        zsum = pltpu.roll(u, rows - 1, 0) + pltpu.roll(u, 1, 0)
        total = jnp.where(has_next, pltpu.roll(u, cells - NY, 1), zero) + jnp.where(
            has_prev, pltpu.roll(u, NY, 1), zero
        )
        plus = jnp.where(has_plus, pltpu.roll(u, cells - 1, 1), zero)
        minus = jnp.where(has_minus, pltpu.roll(u, 1, 1), zero)
        side = total + plus + minus
        return u + rate * (zsum + side - 6.0 * u)

    radius = jnp.zeros((rows, cells), jnp.float32)
    for f in range(ext_ref.shape[0]):
        moved = step(step(ext_ref[f]))
        if f == 0:
            centre_ref[...] = moved
        else:
            radius = radius + jnp.abs(moved)
        moved_ref[pl.ds(f * rows, rows), :] = moved
    radius_ref[...] = radius
    prod_ref[...] = lax.dot_general(
        bank_ref[...],
        moved_ref[...],
        (((1,), (1,)), ((), ())),
        precision=lax.Precision.HIGHEST,
        preferred_element_type=jnp.float32,
    )


def fused_stencil(ext, rate_ext, bank):
    count, rows, cells = ext.shape
    vmem = pl.BlockSpec(memory_space=pltpu.VMEM)
    return pl.pallas_call(
        stencil_kernel,
        out_shape=(
            jax.ShapeDtypeStruct((rows, cells), jnp.float32),
            jax.ShapeDtypeStruct((rows, cells), jnp.float32),
            jax.ShapeDtypeStruct((bank.shape[0], count * rows), jnp.float32),
        ),
        in_specs=[vmem, vmem, vmem],
        out_specs=(vmem, vmem, vmem),
        scratch_shapes=[pltpu.VMEM((count * rows, cells), jnp.float32)],
    )(ext, rate_ext, bank)


def per_device(center, generators, conductivity, cond_table, direction_bank, selection):
    rate_field = lookup_rate(conductivity, cond_table)
    body = jnp.concatenate([center[None], generators], axis=0)
    size = lax.axis_size("slab")
    up = [(i, i + 1) for i in range(size - 1)]
    down = [(j, i) for i, j in up]
    planes = body.shape[1]
    lower = jnp.concatenate([body[:, :2], rate_field[None, :2]], axis=0)
    upper = jnp.concatenate([body[:, planes - 2 :], rate_field[None, planes - 2 :]], axis=0)
    before = lax.ppermute(upper, "slab", up)
    after = lax.ppermute(lower, "slab", down)
    fields = jnp.concatenate([before[:-1], body, after[:-1]], axis=1)
    rate_ext = jnp.concatenate([before[-1], rate_field, after[-1]], axis=0)
    bank_rows = direction_bank.reshape(-1, direction_bank.shape[2])
    centre_ext, radius_ext, prod = fused_stencil(fields, rate_ext, bank_rows)
    centre_moved = centre_ext[2 : 2 + planes]
    radius_local = radius_ext[2 : 2 + planes]
    prod = prod.reshape(direction_bank.shape[0], planes, fields.shape[0], fields.shape[1])
    all_proj = prod[:, 0, :, 2]
    for z in range(1, planes):
        all_proj = all_proj + prod[:, z, :, 2 + z]
    summed = exchange_sum(all_proj, "slab")
    summed_centre, summed_proj = summed[:, 0], summed[:, 1:]
    partial_value = jnp.sum(jnp.abs(summed_proj), axis=1)
    radius, magnitude = exchange_scatter(radius_local, partial_value, "gen")
    columns = radius.shape[1]
    centre_cols = lax.dynamic_slice_in_dim(
        centre_moved, lax.axis_index("gen") * columns, columns, 1
    )
    hull_lo = centre_cols - radius
    hull_hi = centre_cols + radius
    bank_support = summed_centre + magnitude
    supports = select_rows(selection, bank_support)
    return (hull_lo, hull_hi, supports)


def solution(mesh):
    in_specs = (
        P("slab", None),
        P("gen", "slab", None),
        P("slab", None),
        P(),
        P(None, "slab", None),
        P(),
    )
    out_specs = (P("slab", "gen"), P("slab", "gen"), P())
    return jax.shard_map(
        per_device, mesh=mesh, in_specs=in_specs, out_specs=out_specs, check_vma=False
    )
```

```python
import jax
import jax.numpy as jnp
from jax import lax
from jax.sharding import PartitionSpec as P

NX = 64
NY = 64


TIME_STEP = 0.16


def padded_2(x, sides, width):
    for axis, dim in sides:
        size, length = (lax.axis_size(axis), x.shape[dim])
        up = [(i, (i + 1) % size) for i in range(size - 1)]
        down = [(j, i) for i, j in up]
        last = lax.slice_in_dim(x, length - width, length, axis=dim)
        leading = lax.slice_in_dim(x, 0, width, axis=dim)
        before = lax.ppermute(last, axis, up)
        after = lax.ppermute(leading, axis, down)
        x = jnp.concatenate([before, x, after], axis=dim)
    return x


def lookup_rate(conductivity, cond_table):
    classes = jnp.arange(cond_table.shape[0], dtype=jnp.int32)
    picked = jnp.where(
        conductivity[None] == classes[:, None, None], cond_table[:, None, None], jnp.float32(0.0)
    )
    return TIME_STEP * jnp.sum(picked, axis=0)


def lateral(middle):
    cells = NX * NY
    column = jnp.arange(cells, dtype=jnp.int32) % NY
    widths = [(0, 0)] * (middle.ndim - 1) + [(NY, NY)]
    padded = jnp.pad(middle, widths)
    total = padded[..., 2 * NY :] + padded[..., :cells]
    plus = jnp.where(column < NY - 1, padded[..., NY + 1 : NY + 1 + cells], jnp.float32(0.0))
    minus = jnp.where(column > 0, padded[..., NY - 1 : NY - 1 + cells], jnp.float32(0.0))
    return total + plus + minus


def update(extended, rate_field):
    middle = extended[:, 1:-1]
    zsum = extended[:, 2:] + extended[:, :-2]
    return middle + rate_field * (zsum + lateral(middle) - 6.0 * middle)


def select_rows(selection, values):
    entries = jnp.arange(values.shape[0], dtype=jnp.int32)
    return jnp.sum(
        jnp.where(selection[:, None] == entries[None, :], values[None, :], jnp.float32(0.0)), axis=1
    )


def exchange_sum(x, axis):
    size = lax.axis_size(axis)
    flat = x.reshape(-1)
    copies = jnp.broadcast_to(flat[None], (size, flat.shape[0]))
    received = lax.all_to_all(copies, axis, 0, 0, tiled=True)
    return jnp.sum(received, axis=0).reshape(x.shape)


def exchange_scatter(x, extra, axis):
    size = lax.axis_size(axis)
    rows, cols = x.shape
    width = cols // size
    blocks = x.reshape(rows, size, width)
    padded = jnp.pad(extra, (0, width - extra.shape[0]))
    extras = jnp.broadcast_to(padded[None, None], (1, size, width))
    message = jnp.concatenate([blocks, extras], axis=0)
    received = jnp.sum(lax.all_to_all(message, axis, 1, 1, tiled=True), axis=1)
    return received[:rows], received[rows, : extra.shape[0]]


def per_device(center, generators, conductivity, cond_table, direction_bank, selection):
    rate_field = lookup_rate(conductivity, cond_table)
    body = jnp.concatenate([center[None], generators], axis=0)
    size = lax.axis_size("slab")
    up = [(i, i + 1) for i in range(size - 1)]
    down = [(j, i) for i, j in up]
    planes = body.shape[1]
    lower = jnp.concatenate([body[:, :2], rate_field[None, :2]], axis=0)
    upper = jnp.concatenate([body[:, planes - 2 :], rate_field[None, planes - 2 :]], axis=0)
    before = lax.ppermute(upper, "slab", up)
    after = lax.ppermute(lower, "slab", down)
    fields = jnp.concatenate([before[:-1], body, after[:-1]], axis=1)
    rate_ext = jnp.concatenate([before[-1, 1:], rate_field, after[-1, :1]], axis=0)
    fields = update(fields, rate_ext)
    fields = update(fields, rate_field)
    centre_moved = fields[0]
    gens_moved = fields[1:]
    radius_local = jnp.sum(jnp.abs(gens_moved), axis=0)
    all_proj = jnp.einsum(
        "bzc,gzc->bg", direction_bank, fields, precision=lax.Precision.HIGH
    )
    summed = exchange_sum(all_proj, "slab")
    summed_centre, summed_proj = summed[:, 0], summed[:, 1:]
    partial_value = jnp.sum(jnp.abs(summed_proj), axis=1)
    radius, magnitude = exchange_scatter(radius_local, partial_value, "gen")
    columns = radius.shape[1]
    centre_cols = lax.dynamic_slice_in_dim(
        centre_moved, lax.axis_index("gen") * columns, columns, 1
    )
    hull_lo = centre_cols - radius
    hull_hi = centre_cols + radius
    bank_support = summed_centre + magnitude
    supports = select_rows(selection, bank_support)
    return (hull_lo, hull_hi, supports)


def solution(mesh):
    in_specs = (
        P("slab", None),
        P("gen", "slab", None),
        P("slab", None),
        P(),
        P(None, "slab", None),
        P(),
    )
    out_specs = (P("slab", "gen"), P("slab", "gen"), P())
    return jax.shard_map(
        per_device, mesh=mesh, in_specs=in_specs, out_specs=out_specs, check_vma=False
    )
```

```python
import jax
import jax.numpy as jnp
from jax import lax
from jax.sharding import PartitionSpec as P

NX = 64
NY = 64


TIME_STEP = 0.16


def padded_2(x, sides, width):
    for axis, dim in sides:
        size, length = (lax.axis_size(axis), x.shape[dim])
        up = [(i, (i + 1) % size) for i in range(size - 1)]
        down = [(j, i) for i, j in up]
        last = lax.slice_in_dim(x, length - width, length, axis=dim)
        leading = lax.slice_in_dim(x, 0, width, axis=dim)
        before = lax.ppermute(last, axis, up)
        after = lax.ppermute(leading, axis, down)
        x = jnp.concatenate([before, x, after], axis=dim)
    return x


def lookup_rate(conductivity, cond_table):
    classes = jnp.arange(cond_table.shape[0], dtype=jnp.int32)
    picked = jnp.where(
        conductivity[None] == classes[:, None, None], cond_table[:, None, None], jnp.float32(0.0)
    )
    return TIME_STEP * jnp.sum(picked, axis=0)


def lateral(middle):
    cells = NX * NY
    column = jnp.arange(cells, dtype=jnp.int32) % NY
    widths = [(0, 0)] * (middle.ndim - 1) + [(NY, NY)]
    padded = jnp.pad(middle, widths)
    total = padded[..., 2 * NY :] + padded[..., :cells]
    plus = jnp.where(column < NY - 1, padded[..., NY + 1 : NY + 1 + cells], jnp.float32(0.0))
    minus = jnp.where(column > 0, padded[..., NY - 1 : NY - 1 + cells], jnp.float32(0.0))
    return total + plus + minus


def update(extended, rate_field):
    middle = extended[:, 1:-1]
    zsum = extended[:, 2:] + extended[:, :-2]
    return middle + rate_field * (zsum + lateral(middle) - 6.0 * middle)


def select_rows(selection, values):
    entries = jnp.arange(values.shape[0], dtype=jnp.int32)
    return jnp.sum(
        jnp.where(selection[:, None] == entries[None, :], values[None, :], jnp.float32(0.0)), axis=1
    )


def exchange_sum(x, axis):
    size = lax.axis_size(axis)
    flat = x.reshape(-1)
    copies = jnp.broadcast_to(flat[None], (size, flat.shape[0]))
    received = lax.all_to_all(copies, axis, 0, 0, tiled=True)
    return jnp.sum(received, axis=0).reshape(x.shape)


def exchange_scatter(x, extra, axis):
    size = lax.axis_size(axis)
    rows, cols = x.shape
    width = cols // size
    blocks = x.reshape(rows, size, width).transpose(1, 0, 2).reshape(size, rows * width)
    extras = jnp.broadcast_to(extra[None], (size, extra.shape[0]))
    message = jnp.concatenate([blocks, extras], axis=1)
    received = jnp.sum(lax.all_to_all(message, axis, 0, 0, tiled=True), axis=0)
    return received[: rows * width].reshape(rows, width), received[rows * width :]


def per_device(center, generators, conductivity, cond_table, direction_bank, selection):
    rate_field = lookup_rate(conductivity, cond_table)
    body = jnp.concatenate([center[None], generators], axis=0)
    size = lax.axis_size("slab")
    up = [(i, i + 1) for i in range(size - 1)]
    down = [(j, i) for i, j in up]
    planes = body.shape[1]
    lower = jnp.concatenate([body[:, :2], rate_field[None, :2]], axis=0)
    upper = jnp.concatenate([body[:, planes - 2 :], rate_field[None, planes - 2 :]], axis=0)
    before = lax.ppermute(upper, "slab", up)
    after = lax.ppermute(lower, "slab", down)
    fields = jnp.concatenate([before[:-1], body, after[:-1]], axis=1)
    rate_ext = jnp.concatenate([before[-1, 1:], rate_field, after[-1, :1]], axis=0)
    fields = update(fields, rate_ext)
    fields = update(fields, rate_field)
    centre_moved = fields[0]
    gens_moved = fields[1:]
    radius_local = jnp.sum(jnp.abs(gens_moved), axis=0)
    all_proj = jnp.einsum(
        "bzc,gzc->bg", direction_bank, fields, precision=lax.Precision.HIGH
    )
    summed = exchange_sum(all_proj, "slab")
    summed_centre, summed_proj = summed[:, 0], summed[:, 1:]
    partial_value = jnp.sum(jnp.abs(summed_proj), axis=1)
    radius, magnitude = exchange_scatter(radius_local, partial_value, "gen")
    columns = radius.shape[1]
    centre_cols = lax.dynamic_slice_in_dim(
        centre_moved, lax.axis_index("gen") * columns, columns, 1
    )
    hull_lo = centre_cols - radius
    hull_hi = centre_cols + radius
    bank_support = summed_centre + magnitude
    supports = select_rows(selection, bank_support)
    return (hull_lo, hull_hi, supports)


def solution(mesh):
    in_specs = (
        P("slab", None),
        P("gen", "slab", None),
        P("slab", None),
        P(),
        P(None, "slab", None),
        P(),
    )
    out_specs = (P("slab", "gen"), P("slab", "gen"), P())
    return jax.shard_map(
        per_device, mesh=mesh, in_specs=in_specs, out_specs=out_specs, check_vma=False
    )
```

```python
import jax
import jax.numpy as jnp
from jax import lax
from jax.sharding import PartitionSpec as P

NX = 64
NY = 64


TIME_STEP = 0.16


def padded_2(x, sides, width):
    for axis, dim in sides:
        size, length = (lax.axis_size(axis), x.shape[dim])
        up = [(i, (i + 1) % size) for i in range(size - 1)]
        down = [(j, i) for i, j in up]
        last = lax.slice_in_dim(x, length - width, length, axis=dim)
        leading = lax.slice_in_dim(x, 0, width, axis=dim)
        before = lax.ppermute(last, axis, up)
        after = lax.ppermute(leading, axis, down)
        x = jnp.concatenate([before, x, after], axis=dim)
    return x


def lookup_rate(conductivity, cond_table):
    classes = jnp.arange(cond_table.shape[0], dtype=jnp.int32)
    picked = jnp.where(
        conductivity[None] == classes[:, None, None], cond_table[:, None, None], jnp.float32(0.0)
    )
    return TIME_STEP * jnp.sum(picked, axis=0)


def lateral(middle):
    cells = NX * NY
    column = jnp.arange(cells, dtype=jnp.int32) % NY
    widths = [(0, 0)] * (middle.ndim - 1) + [(NY, NY)]
    padded = jnp.pad(middle, widths)
    total = padded[..., 2 * NY :] + padded[..., :cells]
    plus = jnp.where(column < NY - 1, padded[..., NY + 1 : NY + 1 + cells], jnp.float32(0.0))
    minus = jnp.where(column > 0, padded[..., NY - 1 : NY - 1 + cells], jnp.float32(0.0))
    return total + plus + minus


def update(extended, rate_field):
    middle = extended[:, 1:-1]
    zsum = extended[:, 2:] + extended[:, :-2]
    return middle + rate_field * (zsum + lateral(middle) - 6.0 * middle)


def select_rows(selection, values):
    entries = jnp.arange(values.shape[0], dtype=jnp.int32)
    return jnp.sum(
        jnp.where(selection[:, None] == entries[None, :], values[None, :], jnp.float32(0.0)), axis=1
    )


def exchange_sum(x, axis):
    size = lax.axis_size(axis)
    copies = jnp.broadcast_to(x[None], (size,) + x.shape)
    received = lax.all_to_all(copies, axis, 0, 0, tiled=False)
    return jnp.sum(received, axis=0)


def exchange_scatter(x, extra, axis):
    size = lax.axis_size(axis)
    rows, cols = x.shape
    width = cols // size
    blocks = x.reshape(rows, size, width).transpose(1, 0, 2).reshape(size, rows * width)
    extras = jnp.broadcast_to(extra[None], (size, extra.shape[0]))
    message = jnp.concatenate([blocks, extras], axis=1)
    received = jnp.sum(lax.all_to_all(message, axis, 0, 0, tiled=True), axis=0)
    return received[: rows * width].reshape(rows, width), received[rows * width :]


def per_device(center, generators, conductivity, cond_table, direction_bank, selection):
    rate_field = lookup_rate(conductivity, cond_table)
    body = jnp.concatenate([center[None], generators], axis=0)
    size = lax.axis_size("slab")
    up = [(i, i + 1) for i in range(size - 1)]
    down = [(j, i) for i, j in up]
    planes = body.shape[1]
    classes = conductivity.astype(jnp.float32)
    lower = jnp.concatenate([body[:, :2], classes[None, :2]], axis=0)
    upper = jnp.concatenate([body[:, planes - 2 :], classes[None, planes - 2 :]], axis=0)
    before = lax.ppermute(upper, "slab", up)
    after = lax.ppermute(lower, "slab", down)
    fields = jnp.concatenate([before[:-1], body, after[:-1]], axis=1)
    edges = jnp.concatenate([before[-1, 1:], after[-1, :1]], axis=0).astype(jnp.int32)
    edge_rate = lookup_rate(edges, cond_table)
    valid = jnp.concatenate(
        [(lax.axis_index("slab") > 0)[None], (lax.axis_index("slab") < size - 1)[None]]
    )
    edge_rate = jnp.where(valid[:, None], edge_rate, jnp.float32(0.0))
    rate_ext = jnp.concatenate([edge_rate[:1], rate_field, edge_rate[1:]], axis=0)
    fields = update(fields, rate_ext)
    fields = update(fields, rate_field)
    centre_moved = fields[0]
    gens_moved = fields[1:]
    radius_local = jnp.sum(jnp.abs(gens_moved), axis=0)
    all_proj = jnp.einsum(
        "bzc,gzc->bg", direction_bank, fields, precision=lax.Precision.HIGH
    )
    summed = exchange_sum(all_proj, "slab")
    summed_centre, summed_proj = summed[:, 0], summed[:, 1:]
    partial_value = jnp.sum(jnp.abs(summed_proj), axis=1)
    radius, magnitude = exchange_scatter(radius_local, partial_value, "gen")
    columns = radius.shape[1]
    centre_cols = lax.dynamic_slice_in_dim(
        centre_moved, lax.axis_index("gen") * columns, columns, 1
    )
    hull_lo = centre_cols - radius
    hull_hi = centre_cols + radius
    bank_support = summed_centre + magnitude
    supports = select_rows(selection, bank_support)
    return (hull_lo, hull_hi, supports)


def solution(mesh):
    in_specs = (
        P("slab", None),
        P("gen", "slab", None),
        P("slab", None),
        P(),
        P(None, "slab", None),
        P(),
    )
    out_specs = (P("slab", "gen"), P("slab", "gen"), P())
    return jax.shard_map(
        per_device, mesh=mesh, in_specs=in_specs, out_specs=out_specs, check_vma=False
    )
```

```python
import jax
import jax.numpy as jnp
from jax import lax
from jax.sharding import PartitionSpec as P

NX = 64
NY = 64


TIME_STEP = 0.16


def padded_2(x, sides, width):
    for axis, dim in sides:
        size, length = (lax.axis_size(axis), x.shape[dim])
        up = [(i, (i + 1) % size) for i in range(size - 1)]
        down = [(j, i) for i, j in up]
        last = lax.slice_in_dim(x, length - width, length, axis=dim)
        leading = lax.slice_in_dim(x, 0, width, axis=dim)
        before = lax.ppermute(last, axis, up)
        after = lax.ppermute(leading, axis, down)
        x = jnp.concatenate([before, x, after], axis=dim)
    return x


def lookup_rate(conductivity, cond_table):
    classes = jnp.arange(cond_table.shape[0], dtype=jnp.int32)
    picked = jnp.where(
        conductivity[None] == classes[:, None, None], cond_table[:, None, None], jnp.float32(0.0)
    )
    return TIME_STEP * jnp.sum(picked, axis=0)


def lateral(middle):
    cells = NX * NY
    column = jnp.arange(cells, dtype=jnp.int32) % NY
    widths = [(0, 0)] * (middle.ndim - 1) + [(NY, NY)]
    padded = jnp.pad(middle, widths)
    total = padded[..., 2 * NY :] + padded[..., :cells]
    plus = jnp.where(column < NY - 1, padded[..., NY + 1 : NY + 1 + cells], jnp.float32(0.0))
    minus = jnp.where(column > 0, padded[..., NY - 1 : NY - 1 + cells], jnp.float32(0.0))
    return total + plus + minus


def update(extended, rate_field):
    middle = extended[:, 1:-1]
    zsum = extended[:, 2:] + extended[:, :-2]
    return middle + rate_field * (zsum + lateral(middle) - 6.0 * middle)


def select_rows(selection, values):
    entries = jnp.arange(values.shape[0], dtype=jnp.int32)
    return jnp.sum(
        jnp.where(selection[:, None] == entries[None, :], values[None, :], jnp.float32(0.0)), axis=1
    )


def exchange_sum(x, axis):
    size = lax.axis_size(axis)
    copies = jnp.broadcast_to(x[None], (size,) + x.shape)
    received = lax.all_to_all(copies, axis, 0, 0, tiled=False)
    return jnp.sum(received, axis=0)


def exchange_scatter(x, extra, axis):
    size = lax.axis_size(axis)
    rows, cols = x.shape
    width = cols // size
    blocks = x.reshape(rows, size, width).transpose(1, 0, 2).reshape(size, rows * width)
    extras = jnp.broadcast_to(extra[None], (size, extra.shape[0]))
    message = jnp.concatenate([blocks, extras], axis=1)
    received = jnp.sum(lax.all_to_all(message, axis, 0, 0, tiled=True), axis=0)
    return received[: rows * width].reshape(rows, width), received[rows * width :]


def per_device(center, generators, conductivity, cond_table, direction_bank, selection):
    rate_field = lookup_rate(conductivity, cond_table)
    body = jnp.concatenate([center[None], generators], axis=0)
    size = lax.axis_size("slab")
    up = [(i, i + 1) for i in range(size - 1)]
    down = [(j, i) for i, j in up]
    planes = body.shape[1]
    lower = jnp.concatenate([body[:, :2], rate_field[None, :2]], axis=0)
    upper = jnp.concatenate([body[:, planes - 2 :], rate_field[None, planes - 2 :]], axis=0)
    before = lax.ppermute(upper, "slab", up)
    after = lax.ppermute(lower, "slab", down)
    fields = jnp.concatenate([before[:-1], body, after[:-1]], axis=1)
    rate_ext = jnp.concatenate([before[-1, 1:], rate_field, after[-1, :1]], axis=0)
    fields = update(fields, rate_ext)
    fields = update(fields, rate_field)
    centre_moved = fields[0]
    gens_moved = fields[1:]
    radius_local = jnp.sum(jnp.abs(gens_moved), axis=0)
    all_proj = jnp.einsum(
        "bzc,gzc->bg", direction_bank, fields, precision=lax.Precision.HIGHEST
    )
    summed = exchange_sum(all_proj, "slab")
    summed_centre, summed_proj = summed[:, 0], summed[:, 1:]
    partial_value = jnp.sum(jnp.abs(summed_proj), axis=1)
    radius, magnitude = exchange_scatter(radius_local, partial_value, "gen")
    columns = radius.shape[1]
    centre_cols = lax.dynamic_slice_in_dim(
        centre_moved, lax.axis_index("gen") * columns, columns, 1
    )
    hull_lo = centre_cols - radius
    hull_hi = centre_cols + radius
    bank_support = summed_centre + magnitude
    supports = select_rows(selection, bank_support)
    return (hull_lo, hull_hi, supports)


def solution(mesh):
    in_specs = (
        P("slab", None),
        P("gen", "slab", None),
        P("slab", None),
        P(),
        P(None, "slab", None),
        P(),
    )
    out_specs = (P("slab", "gen"), P("slab", "gen"), P())
    return jax.shard_map(
        per_device, mesh=mesh, in_specs=in_specs, out_specs=out_specs, check_vma=False
    )
```

```python
import jax
import jax.numpy as jnp
from jax import lax
from jax.sharding import PartitionSpec as P

NX = 64
NY = 64


TIME_STEP = 0.16


def padded_2(x, sides, width):
    for axis, dim in sides:
        size, length = (lax.axis_size(axis), x.shape[dim])
        up = [(i, (i + 1) % size) for i in range(size - 1)]
        down = [(j, i) for i, j in up]
        last = lax.slice_in_dim(x, length - width, length, axis=dim)
        leading = lax.slice_in_dim(x, 0, width, axis=dim)
        before = lax.ppermute(last, axis, up)
        after = lax.ppermute(leading, axis, down)
        x = jnp.concatenate([before, x, after], axis=dim)
    return x


def lookup_rate(conductivity, cond_table):
    classes = jnp.arange(cond_table.shape[0], dtype=jnp.int32)
    picked = jnp.where(
        conductivity[None] == classes[:, None, None], cond_table[:, None, None], jnp.float32(0.0)
    )
    return TIME_STEP * jnp.sum(picked, axis=0)


def lateral(middle):
    cells = NX * NY
    column = jnp.arange(cells, dtype=jnp.int32) % NY
    widths = [(0, 0)] * (middle.ndim - 1) + [(NY, NY)]
    padded = jnp.pad(middle, widths)
    total = padded[..., 2 * NY :] + padded[..., :cells]
    plus = jnp.where(column < NY - 1, padded[..., NY + 1 : NY + 1 + cells], jnp.float32(0.0))
    minus = jnp.where(column > 0, padded[..., NY - 1 : NY - 1 + cells], jnp.float32(0.0))
    return total + plus + minus


def update(extended, rate_field):
    middle = extended[:, 1:-1]
    zsum = extended[:, 2:] + extended[:, :-2]
    return middle + rate_field * (zsum + lateral(middle) - 6.0 * middle)


def select_rows(selection, values):
    entries = jnp.arange(values.shape[0], dtype=jnp.int32)
    return jnp.sum(
        jnp.where(selection[:, None] == entries[None, :], values[None, :], jnp.float32(0.0)), axis=1
    )


def exchange_sum(x, axis):
    size = lax.axis_size(axis)
    copies = jnp.broadcast_to(x[None], (size,) + x.shape)
    received = lax.all_to_all(copies, axis, 0, 0, tiled=False)
    return jnp.sum(received, axis=0)


def exchange_scatter(x, extra, axis):
    size = lax.axis_size(axis)
    rows, cols = x.shape
    width = cols // size
    blocks = x.reshape(rows, size, width).transpose(1, 0, 2).reshape(size, rows * width)
    extras = jnp.broadcast_to(extra[None], (size, extra.shape[0]))
    message = jnp.concatenate([blocks, extras], axis=1)
    received = jnp.sum(lax.all_to_all(message, axis, 0, 0, tiled=True), axis=0)
    return received[: rows * width].reshape(rows, width), received[rows * width :]


def per_device(center, generators, conductivity, cond_table, direction_bank, selection):
    rate_field = lookup_rate(conductivity, cond_table)
    body = jnp.concatenate([center[None], generators], axis=0)
    size = lax.axis_size("slab")
    up = [(i, i + 1) for i in range(size - 1)]
    down = [(j, i) for i, j in up]
    planes = body.shape[1]
    lower = jnp.concatenate([body[:, :2], rate_field[None, :2]], axis=0)
    upper = jnp.concatenate([body[:, planes - 2 :], rate_field[None, planes - 2 :]], axis=0)
    even = lax.axis_index("slab") % 2 == 0
    across = [(i, i + 1) for i in range(1, size - 1, 2)] + [(i, i - 1) for i in range(2, size, 2)]
    within = [(i, i + 1) for i in range(0, size, 2)] + [(i + 1, i) for i in range(0, size, 2)]
    far = lax.ppermute(jnp.where(even, lower, upper), "slab", across)
    near = lax.ppermute(jnp.where(even, upper, lower), "slab", within)
    before = jnp.where(even, far, near)
    after = jnp.where(even, near, far)
    fields = jnp.concatenate([before[:-1], body, after[:-1]], axis=1)
    rate_ext = jnp.concatenate([before[-1, 1:], rate_field, after[-1, :1]], axis=0)
    fields = update(fields, rate_ext)
    fields = update(fields, rate_field)
    centre_moved = fields[0]
    gens_moved = fields[1:]
    radius_local = jnp.sum(jnp.abs(gens_moved), axis=0)
    all_proj = jnp.einsum(
        "bzc,gzc->bg", direction_bank, fields, precision=lax.Precision.HIGHEST
    )
    summed = exchange_sum(all_proj, "slab")
    summed_centre, summed_proj = summed[:, 0], summed[:, 1:]
    partial_value = jnp.sum(jnp.abs(summed_proj), axis=1)
    radius, magnitude = exchange_scatter(radius_local, partial_value, "gen")
    columns = radius.shape[1]
    centre_cols = lax.dynamic_slice_in_dim(
        centre_moved, lax.axis_index("gen") * columns, columns, 1
    )
    hull_lo = centre_cols - radius
    hull_hi = centre_cols + radius
    bank_support = summed_centre + magnitude
    supports = select_rows(selection, bank_support)
    return (hull_lo, hull_hi, supports)


def solution(mesh):
    in_specs = (
        P("slab", None),
        P("gen", "slab", None),
        P("slab", None),
        P(),
        P(None, "slab", None),
        P(),
    )
    out_specs = (P("slab", "gen"), P("slab", "gen"), P())
    return jax.shard_map(
        per_device, mesh=mesh, in_specs=in_specs, out_specs=out_specs, check_vma=False
    )
```

```python
import jax
import jax.numpy as jnp
from jax import lax
from jax.sharding import PartitionSpec as P

NX = 64
NY = 64


TIME_STEP = 0.16


def padded_2(x, sides, width):
    for axis, dim in sides:
        size, length = (lax.axis_size(axis), x.shape[dim])
        up = [(i, (i + 1) % size) for i in range(size - 1)]
        down = [(j, i) for i, j in up]
        last = lax.slice_in_dim(x, length - width, length, axis=dim)
        leading = lax.slice_in_dim(x, 0, width, axis=dim)
        before = lax.ppermute(last, axis, up)
        after = lax.ppermute(leading, axis, down)
        x = jnp.concatenate([before, x, after], axis=dim)
    return x


def lookup_rate(conductivity, cond_table):
    classes = jnp.arange(cond_table.shape[0], dtype=jnp.int32)
    picked = jnp.where(
        conductivity[None] == classes[:, None, None], cond_table[:, None, None], jnp.float32(0.0)
    )
    return TIME_STEP * jnp.sum(picked, axis=0)


def lateral(middle):
    cells = NX * NY
    column = jnp.arange(cells, dtype=jnp.int32) % NY
    widths = [(0, 0)] * (middle.ndim - 1) + [(NY, NY)]
    padded = jnp.pad(middle, widths)
    total = padded[..., 2 * NY :] + padded[..., :cells]
    plus = jnp.where(column < NY - 1, padded[..., NY + 1 : NY + 1 + cells], jnp.float32(0.0))
    minus = jnp.where(column > 0, padded[..., NY - 1 : NY - 1 + cells], jnp.float32(0.0))
    return total + plus + minus


def update(extended, rate_field):
    middle = extended[:, 1:-1]
    zsum = extended[:, 2:] + extended[:, :-2]
    return middle + rate_field * (zsum + lateral(middle) - 6.0 * middle)


def select_rows(selection, values):
    entries = jnp.arange(values.shape[0], dtype=jnp.int32)
    return jnp.sum(
        jnp.where(selection[:, None] == entries[None, :], values[None, :], jnp.float32(0.0)), axis=1
    )


def exchange_sum(x, axis):
    size = lax.axis_size(axis)
    copies = jnp.broadcast_to(x[None], (size,) + x.shape)
    received = lax.all_to_all(copies, axis, 0, 0, tiled=False)
    return jnp.sum(received, axis=0)


def exchange_scatter(x, extra, axis):
    size = lax.axis_size(axis)
    rows, cols = x.shape
    width = cols // size
    blocks = x.reshape(rows, size, width).transpose(1, 0, 2).reshape(size, rows * width)
    extras = jnp.broadcast_to(extra[None], (size, extra.shape[0]))
    message = jnp.concatenate([blocks, extras], axis=1)
    received = jnp.sum(lax.all_to_all(message, axis, 0, 0, tiled=True), axis=0)
    return received[: rows * width].reshape(rows, width), received[rows * width :]


def per_device(center, generators, conductivity, cond_table, direction_bank, selection):
    rate_field = lookup_rate(conductivity, cond_table)
    body = jnp.concatenate([center[None], generators], axis=0)
    size = lax.axis_size("slab")
    up = [(i, i + 1) for i in range(size - 1)]
    down = [(j, i) for i, j in up]
    planes = body.shape[1]
    lower = jnp.concatenate([body[:, :2], rate_field[None, :2]], axis=0)
    upper = jnp.concatenate([body[:, planes - 2 :], rate_field[None, planes - 2 :]], axis=0)
    even = lax.axis_index("slab") % 2 == 0
    across = [(i, i + 1) for i in range(1, size - 1, 2)] + [(i, i - 1) for i in range(2, size, 2)]
    within = [(i, i + 1) for i in range(0, size, 2)] + [(i + 1, i) for i in range(0, size, 2)]
    outgoing = jnp.where(even, lower, upper)
    split = (body.shape[0] + 1) // 2
    first = jnp.concatenate([outgoing[:split], outgoing[-1:]], axis=0)
    far_first = lax.ppermute(first, "slab", across)
    near = lax.ppermute(jnp.where(even, upper, lower), "slab", within)
    second, near = lax.optimization_barrier((outgoing[split:-1], near))
    far_second = lax.ppermute(second, "slab", across)
    near_first = jnp.concatenate([near[:split], near[-1:]], axis=0)
    rate_far = far_first[-1]
    rate_before = jnp.where(even, rate_far, near[-1])
    rate_after = jnp.where(even, near[-1], rate_far)
    rate_ext = jnp.concatenate([rate_before[1:], rate_field, rate_after[:1]], axis=0)

    def advance_part(part, far):
        before = jnp.where(even, far, near[part])
        after = jnp.where(even, near[part], far)
        fields = jnp.concatenate([before, body[part], after], axis=1)
        fields = update(fields, rate_ext)
        fields = update(fields, rate_field)
        proj = jnp.einsum(
            "bzc,gzc->bg", direction_bank, fields, precision=lax.Precision.HIGHEST
        )
        return fields, proj

    moved_first, proj_first = advance_part(slice(0, split), far_first[:-1])
    far_second, proj_first, moved_first = lax.optimization_barrier(
        (far_second, proj_first, moved_first)
    )
    moved_second, proj_second = advance_part(slice(split, body.shape[0]), far_second)
    centre_moved = moved_first[0]
    radius_local = jnp.sum(jnp.abs(moved_first[1:]), axis=0) + jnp.sum(
        jnp.abs(moved_second), axis=0
    )
    all_proj = jnp.concatenate([proj_first, proj_second], axis=1)
    summed = exchange_sum(all_proj, "slab")
    summed_centre, summed_proj = summed[:, 0], summed[:, 1:]
    partial_value = jnp.sum(jnp.abs(summed_proj), axis=1)
    radius, magnitude = exchange_scatter(radius_local, partial_value, "gen")
    columns = radius.shape[1]
    centre_cols = lax.dynamic_slice_in_dim(
        centre_moved, lax.axis_index("gen") * columns, columns, 1
    )
    hull_lo = centre_cols - radius
    hull_hi = centre_cols + radius
    bank_support = summed_centre + magnitude
    supports = select_rows(selection, bank_support)
    return (hull_lo, hull_hi, supports)


def solution(mesh):
    in_specs = (
        P("slab", None),
        P("gen", "slab", None),
        P("slab", None),
        P(),
        P(None, "slab", None),
        P(),
    )
    out_specs = (P("slab", "gen"), P("slab", "gen"), P())
    return jax.shard_map(
        per_device, mesh=mesh, in_specs=in_specs, out_specs=out_specs, check_vma=False
    )
```

```python
import jax
import jax.numpy as jnp
from jax import lax
from jax.sharding import PartitionSpec as P

NX = 64
NY = 64


TIME_STEP = 0.16


def padded_2(x, sides, width):
    for axis, dim in sides:
        size, length = (lax.axis_size(axis), x.shape[dim])
        up = [(i, (i + 1) % size) for i in range(size - 1)]
        down = [(j, i) for i, j in up]
        last = lax.slice_in_dim(x, length - width, length, axis=dim)
        leading = lax.slice_in_dim(x, 0, width, axis=dim)
        before = lax.ppermute(last, axis, up)
        after = lax.ppermute(leading, axis, down)
        x = jnp.concatenate([before, x, after], axis=dim)
    return x


def lookup_rate(conductivity, cond_table):
    classes = jnp.arange(cond_table.shape[0], dtype=jnp.int32)
    picked = jnp.where(
        conductivity[None] == classes[:, None, None], cond_table[:, None, None], jnp.float32(0.0)
    )
    return TIME_STEP * jnp.sum(picked, axis=0)


def lateral(middle):
    cells = NX * NY
    column = jnp.arange(cells, dtype=jnp.int32) % NY
    widths = [(0, 0)] * (middle.ndim - 1) + [(NY, NY)]
    padded = jnp.pad(middle, widths)
    total = padded[..., 2 * NY :] + padded[..., :cells]
    plus = jnp.where(column < NY - 1, padded[..., NY + 1 : NY + 1 + cells], jnp.float32(0.0))
    minus = jnp.where(column > 0, padded[..., NY - 1 : NY - 1 + cells], jnp.float32(0.0))
    return total + plus + minus


def update(extended, rate_field):
    middle = extended[:, 1:-1]
    zsum = extended[:, 2:] + extended[:, :-2]
    return middle + rate_field * (zsum + lateral(middle) - 6.0 * middle)


def select_rows(selection, values):
    entries = jnp.arange(values.shape[0], dtype=jnp.int32)
    return jnp.sum(
        jnp.where(selection[:, None] == entries[None, :], values[None, :], jnp.float32(0.0)), axis=1
    )


def exchange_sum(x, axis):
    size = lax.axis_size(axis)
    copies = jnp.broadcast_to(x[None], (size,) + x.shape)
    received = lax.all_to_all(copies, axis, 0, 0, tiled=False)
    return jnp.sum(received, axis=0)


def exchange_scatter(x, extra, axis):
    size = lax.axis_size(axis)
    rows, cols = x.shape
    width = cols // size
    blocks = x.reshape(rows, size, width).transpose(1, 0, 2).reshape(size, rows * width)
    extras = jnp.broadcast_to(extra[None], (size, extra.shape[0]))
    message = jnp.concatenate([blocks, extras], axis=1)
    received = jnp.sum(lax.all_to_all(message, axis, 0, 0, tiled=True), axis=0)
    return received[: rows * width].reshape(rows, width), received[rows * width :]


def per_device(center, generators, conductivity, cond_table, direction_bank, selection):
    rate_field = lookup_rate(conductivity, cond_table)
    body = jnp.concatenate([center[None], generators], axis=0)
    size = lax.axis_size("slab")
    up = [(i, i + 1) for i in range(size - 1)]
    down = [(j, i) for i, j in up]
    planes = body.shape[1]
    lower = jnp.concatenate([body[:, :2], rate_field[None, :2]], axis=0)
    upper = jnp.concatenate([body[:, planes - 2 :], rate_field[None, planes - 2 :]], axis=0)
    even = lax.axis_index("slab") % 2 == 0
    across = [(i, i + 1) for i in range(1, size - 1, 2)] + [(i, i - 1) for i in range(2, size, 2)]
    within = [(i, i + 1) for i in range(0, size, 2)] + [(i + 1, i) for i in range(0, size, 2)]
    outgoing = jnp.where(even, lower, upper)
    split = (body.shape[0] + 1) // 2
    first = jnp.concatenate([outgoing[:split], outgoing[-1:]], axis=0)
    far_first = lax.ppermute(first, "slab", across)
    second, inner, far_first = lax.optimization_barrier(
        (outgoing[split:-1], jnp.where(even, upper, lower), far_first)
    )
    far_second = lax.ppermute(second, "slab", across)
    near = lax.ppermute(inner, "slab", within)
    near_first = jnp.concatenate([near[:split], near[-1:]], axis=0)
    rate_far = far_first[-1]
    rate_before = jnp.where(even, rate_far, near[-1])
    rate_after = jnp.where(even, near[-1], rate_far)
    rate_ext = jnp.concatenate([rate_before[1:], rate_field, rate_after[:1]], axis=0)

    def advance_part(part, far):
        before = jnp.where(even, far, near[part])
        after = jnp.where(even, near[part], far)
        fields = jnp.concatenate([before, body[part], after], axis=1)
        fields = update(fields, rate_ext)
        fields = update(fields, rate_field)
        proj = jnp.einsum(
            "bzc,gzc->bg", direction_bank, fields, precision=lax.Precision.HIGHEST
        )
        return fields, proj

    moved_first, proj_first = advance_part(slice(0, split), far_first[:-1])
    far_second, proj_first, moved_first = lax.optimization_barrier(
        (far_second, proj_first, moved_first)
    )
    moved_second, proj_second = advance_part(slice(split, body.shape[0]), far_second)
    centre_moved = moved_first[0]
    radius_local = jnp.sum(jnp.abs(moved_first[1:]), axis=0) + jnp.sum(
        jnp.abs(moved_second), axis=0
    )
    all_proj = jnp.concatenate([proj_first, proj_second], axis=1)
    summed = exchange_sum(all_proj, "slab")
    summed_centre, summed_proj = summed[:, 0], summed[:, 1:]
    partial_value = jnp.sum(jnp.abs(summed_proj), axis=1)
    radius, magnitude = exchange_scatter(radius_local, partial_value, "gen")
    columns = radius.shape[1]
    centre_cols = lax.dynamic_slice_in_dim(
        centre_moved, lax.axis_index("gen") * columns, columns, 1
    )
    hull_lo = centre_cols - radius
    hull_hi = centre_cols + radius
    bank_support = summed_centre + magnitude
    supports = select_rows(selection, bank_support)
    return (hull_lo, hull_hi, supports)


def solution(mesh):
    in_specs = (
        P("slab", None),
        P("gen", "slab", None),
        P("slab", None),
        P(),
        P(None, "slab", None),
        P(),
    )
    out_specs = (P("slab", "gen"), P("slab", "gen"), P())
    return jax.shard_map(
        per_device, mesh=mesh, in_specs=in_specs, out_specs=out_specs, check_vma=False
    )
```

```python
import jax
import jax.numpy as jnp
from jax import lax
from jax.sharding import PartitionSpec as P

NX = 64
NY = 64


TIME_STEP = 0.16


def padded_2(x, sides, width):
    for axis, dim in sides:
        size, length = (lax.axis_size(axis), x.shape[dim])
        up = [(i, (i + 1) % size) for i in range(size - 1)]
        down = [(j, i) for i, j in up]
        last = lax.slice_in_dim(x, length - width, length, axis=dim)
        leading = lax.slice_in_dim(x, 0, width, axis=dim)
        before = lax.ppermute(last, axis, up)
        after = lax.ppermute(leading, axis, down)
        x = jnp.concatenate([before, x, after], axis=dim)
    return x


def lookup_rate(conductivity, cond_table):
    picked = jnp.full(conductivity.shape, cond_table[0], jnp.float32)
    for k in range(1, cond_table.shape[0]):
        picked = jnp.where(conductivity == k, cond_table[k], picked)
    return TIME_STEP * picked


def lateral(middle):
    cells = NX * NY
    column = jnp.arange(cells, dtype=jnp.int32) % NY
    widths = [(0, 0)] * (middle.ndim - 1) + [(NY, NY)]
    padded = jnp.pad(middle, widths)
    total = padded[..., 2 * NY :] + padded[..., :cells]
    plus = jnp.where(column < NY - 1, padded[..., NY + 1 : NY + 1 + cells], jnp.float32(0.0))
    minus = jnp.where(column > 0, padded[..., NY - 1 : NY - 1 + cells], jnp.float32(0.0))
    return total + plus + minus


def update(extended, rate_field):
    middle = extended[:, 1:-1]
    zsum = extended[:, 2:] + extended[:, :-2]
    return middle + rate_field * (zsum + lateral(middle) - 6.0 * middle)


def select_rows(selection, values):
    entries = jnp.arange(values.shape[0], dtype=jnp.int32)
    return jnp.sum(
        jnp.where(selection[:, None] == entries[None, :], values[None, :], jnp.float32(0.0)), axis=1
    )


def exchange_sum(x, axis):
    size = lax.axis_size(axis)
    copies = jnp.broadcast_to(x[None], (size,) + x.shape)
    received = lax.all_to_all(copies, axis, 0, 0, tiled=False)
    return jnp.sum(received, axis=0)


def exchange_scatter(x, extra, axis):
    size = lax.axis_size(axis)
    rows, cols = x.shape
    width = cols // size
    blocks = x.reshape(rows, size, width).transpose(1, 0, 2).reshape(size, rows * width)
    extras = jnp.broadcast_to(extra[None], (size, extra.shape[0]))
    message = jnp.concatenate([blocks, extras], axis=1)
    received = jnp.sum(lax.all_to_all(message, axis, 0, 0, tiled=True), axis=0)
    return received[: rows * width].reshape(rows, width), received[rows * width :]


def per_device(center, generators, conductivity, cond_table, direction_bank, selection):
    rate_field = lookup_rate(conductivity, cond_table)
    body = jnp.concatenate([center[None], generators], axis=0)
    size = lax.axis_size("slab")
    up = [(i, i + 1) for i in range(size - 1)]
    down = [(j, i) for i, j in up]
    planes = body.shape[1]
    lower = jnp.concatenate([body[:, :2], rate_field[None, :2]], axis=0)
    upper = jnp.concatenate([body[:, planes - 2 :], rate_field[None, planes - 2 :]], axis=0)
    even = lax.axis_index("slab") % 2 == 0
    across = [(i, i + 1) for i in range(1, size - 1, 2)] + [(i, i - 1) for i in range(2, size, 2)]
    within = [(i, i + 1) for i in range(0, size, 2)] + [(i + 1, i) for i in range(0, size, 2)]
    far = lax.ppermute(jnp.where(even, lower, upper), "slab", across)
    near = lax.ppermute(jnp.where(even, upper, lower), "slab", within)
    before = jnp.where(even, far, near)
    after = jnp.where(even, near, far)
    fields = jnp.concatenate([before[:-1], body, after[:-1]], axis=1)
    rate_ext = jnp.concatenate([before[-1, 1:], rate_field, after[-1, :1]], axis=0)
    fields = update(fields, rate_ext)
    fields = update(fields, rate_field)
    centre_moved = fields[0]
    gens_moved = fields[1:]
    radius_local = jnp.sum(jnp.abs(gens_moved), axis=0)
    all_proj = jnp.einsum(
        "bzc,gzc->bg", direction_bank, fields, precision=lax.Precision.HIGHEST
    )
    summed = exchange_sum(all_proj, "slab")
    summed_centre, summed_proj = summed[:, 0], summed[:, 1:]
    partial_value = jnp.sum(jnp.abs(summed_proj), axis=1)
    radius, magnitude = exchange_scatter(radius_local, partial_value, "gen")
    columns = radius.shape[1]
    centre_cols = lax.dynamic_slice_in_dim(
        centre_moved, lax.axis_index("gen") * columns, columns, 1
    )
    hull_lo = centre_cols - radius
    hull_hi = centre_cols + radius
    bank_support = summed_centre + magnitude
    supports = select_rows(selection, bank_support)
    return (hull_lo, hull_hi, supports)


def solution(mesh):
    in_specs = (
        P("slab", None),
        P("gen", "slab", None),
        P("slab", None),
        P(),
        P(None, "slab", None),
        P(),
    )
    out_specs = (P("slab", "gen"), P("slab", "gen"), P())
    return jax.shard_map(
        per_device, mesh=mesh, in_specs=in_specs, out_specs=out_specs, check_vma=False
    )
```

```python
import jax
import jax.numpy as jnp
from jax import lax
from jax.sharding import PartitionSpec as P

NX = 64
NY = 64


TIME_STEP = 0.16


def padded_2(x, sides, width):
    for axis, dim in sides:
        size, length = (lax.axis_size(axis), x.shape[dim])
        up = [(i, (i + 1) % size) for i in range(size - 1)]
        down = [(j, i) for i, j in up]
        last = lax.slice_in_dim(x, length - width, length, axis=dim)
        leading = lax.slice_in_dim(x, 0, width, axis=dim)
        before = lax.ppermute(last, axis, up)
        after = lax.ppermute(leading, axis, down)
        x = jnp.concatenate([before, x, after], axis=dim)
    return x


def lookup_rate(conductivity, cond_table):
    classes = jnp.arange(cond_table.shape[0], dtype=jnp.int32)
    picked = jnp.where(
        conductivity[None] == classes[:, None, None], cond_table[:, None, None], jnp.float32(0.0)
    )
    return TIME_STEP * jnp.sum(picked, axis=0)


def lateral(middle):
    cells = NX * NY
    column = jnp.arange(cells, dtype=jnp.int32) % NY
    widths = [(0, 0)] * (middle.ndim - 1) + [(NY, NY)]
    padded = jnp.pad(middle, widths)
    total = padded[..., 2 * NY :] + padded[..., :cells]
    plus = jnp.where(column < NY - 1, padded[..., NY + 1 : NY + 1 + cells], jnp.float32(0.0))
    minus = jnp.where(column > 0, padded[..., NY - 1 : NY - 1 + cells], jnp.float32(0.0))
    return total + plus + minus


def update(extended, rate_field):
    middle = extended[:, 1:-1]
    zsum = extended[:, 2:] + extended[:, :-2]
    return middle + rate_field * (zsum + lateral(middle) - 6.0 * middle)


def select_rows(selection, values):
    entries = jnp.arange(values.shape[0], dtype=jnp.int32)
    return jnp.sum(
        jnp.where(selection[:, None] == entries[None, :], values[None, :], jnp.float32(0.0)), axis=1
    )


def exchange_sum(x, axis):
    size = lax.axis_size(axis)
    copies = jnp.broadcast_to(x[None], (size,) + x.shape)
    received = lax.all_to_all(copies, axis, 0, 0, tiled=False)
    return jnp.sum(received, axis=0)


def exchange_scatter(x, extra, axis):
    size = lax.axis_size(axis)
    rows, cols = x.shape
    width = cols // size
    blocks = x.reshape(rows, size, width).transpose(1, 0, 2).reshape(size, rows * width)
    extras = jnp.broadcast_to(extra[None], (size, extra.shape[0]))
    message = jnp.concatenate([blocks, extras], axis=1)
    received = jnp.sum(lax.all_to_all(message, axis, 0, 0, tiled=True), axis=0)
    return received[: rows * width].reshape(rows, width), received[rows * width :]


def per_device(center, generators, conductivity, cond_table, direction_bank, selection):
    rate_field = lookup_rate(conductivity, cond_table)
    body = jnp.concatenate([center[None], generators], axis=0)
    size = lax.axis_size("slab")
    up = [(i, i + 1) for i in range(size - 1)]
    down = [(j, i) for i, j in up]
    planes = body.shape[1]
    lower = jnp.concatenate([body[:, :2], rate_field[None, :2]], axis=0)
    upper = jnp.concatenate([body[:, planes - 2 :], rate_field[None, planes - 2 :]], axis=0)
    even = lax.axis_index("slab") % 2 == 0
    across = [(i, i + 1) for i in range(1, size - 1, 2)] + [(i, i - 1) for i in range(2, size, 2)]
    within = [(i, i + 1) for i in range(0, size, 2)] + [(i + 1, i) for i in range(0, size, 2)]
    far = lax.ppermute(jnp.where(even, lower, upper), "slab", across)
    near = lax.ppermute(jnp.where(even, upper, lower), "slab", within)
    before = jnp.where(even, far, near)
    after = jnp.where(even, near, far)
    fields = jnp.concatenate([before[:-1], body, after[:-1]], axis=1)
    rate_ext = jnp.concatenate([before[-1, 1:], rate_field, after[-1, :1]], axis=0)
    centre_moved = update(update(fields[:1], rate_ext), rate_field)[0]
    gens_moved = update(update(fields[1:], rate_ext), rate_field)
    fields = jnp.concatenate([centre_moved[None], gens_moved], axis=0)
    radius_local = jnp.sum(jnp.abs(gens_moved), axis=0)
    all_proj = jnp.einsum(
        "bzc,gzc->bg", direction_bank, fields, precision=lax.Precision.HIGHEST
    )
    summed = exchange_sum(all_proj, "slab")
    summed_centre, summed_proj = summed[:, 0], summed[:, 1:]
    partial_value = jnp.sum(jnp.abs(summed_proj), axis=1)
    radius, magnitude = exchange_scatter(radius_local, partial_value, "gen")
    columns = radius.shape[1]
    centre_cols = lax.dynamic_slice_in_dim(
        centre_moved, lax.axis_index("gen") * columns, columns, 1
    )
    hull_lo = centre_cols - radius
    hull_hi = centre_cols + radius
    bank_support = summed_centre + magnitude
    supports = select_rows(selection, bank_support)
    return (hull_lo, hull_hi, supports)


def solution(mesh):
    in_specs = (
        P("slab", None),
        P("gen", "slab", None),
        P("slab", None),
        P(),
        P(None, "slab", None),
        P(),
    )
    out_specs = (P("slab", "gen"), P("slab", "gen"), P())
    return jax.shard_map(
        per_device, mesh=mesh, in_specs=in_specs, out_specs=out_specs, check_vma=False
    )
```

```python
import jax
import jax.numpy as jnp
from jax import lax
from jax.sharding import PartitionSpec as P

NX = 64
NY = 64


TIME_STEP = 0.16


def padded_2(x, sides, width):
    for axis, dim in sides:
        size, length = (lax.axis_size(axis), x.shape[dim])
        up = [(i, (i + 1) % size) for i in range(size - 1)]
        down = [(j, i) for i, j in up]
        last = lax.slice_in_dim(x, length - width, length, axis=dim)
        leading = lax.slice_in_dim(x, 0, width, axis=dim)
        before = lax.ppermute(last, axis, up)
        after = lax.ppermute(leading, axis, down)
        x = jnp.concatenate([before, x, after], axis=dim)
    return x


def lookup_rate(conductivity, cond_table):
    classes = jnp.arange(cond_table.shape[0], dtype=jnp.int32)
    picked = jnp.where(
        conductivity[None] == classes[:, None, None], cond_table[:, None, None], jnp.float32(0.0)
    )
    return TIME_STEP * jnp.sum(picked, axis=0)


def lateral(middle):
    cells = NX * NY
    column = jnp.arange(cells, dtype=jnp.int32) % NY
    widths = [(0, 0)] * (middle.ndim - 1) + [(NY, NY)]
    padded = jnp.pad(middle, widths)
    total = padded[..., 2 * NY :] + padded[..., :cells]
    plus = jnp.where(column < NY - 1, padded[..., NY + 1 : NY + 1 + cells], jnp.float32(0.0))
    minus = jnp.where(column > 0, padded[..., NY - 1 : NY - 1 + cells], jnp.float32(0.0))
    return total + plus + minus


def update(extended, rate_field):
    middle = extended[:, 1:-1]
    zsum = extended[:, 2:] + extended[:, :-2]
    return middle + rate_field * (zsum + lateral(middle) - 6.0 * middle)


def select_rows(selection, values):
    entries = jnp.arange(values.shape[0], dtype=jnp.int32)
    return jnp.sum(
        jnp.where(selection[:, None] == entries[None, :], values[None, :], jnp.float32(0.0)), axis=1
    )


def exchange_sum(x, axis):
    size = lax.axis_size(axis)
    flat = x.reshape(-1)
    copies = jnp.broadcast_to(flat[None], (size, flat.shape[0]))
    received = lax.all_to_all(copies, axis, 0, 0, tiled=True)
    return jnp.sum(received, axis=0).reshape(x.shape)


def exchange_scatter(x, extra, axis):
    size = lax.axis_size(axis)
    rows, cols = x.shape
    width = cols // size
    blocks = x.reshape(rows, size, width).transpose(1, 0, 2).reshape(size, rows * width)
    extras = jnp.broadcast_to(extra[None], (size, extra.shape[0]))
    message = jnp.concatenate([blocks, extras], axis=1)
    received = jnp.sum(lax.all_to_all(message, axis, 0, 0, tiled=True), axis=0)
    return received[: rows * width].reshape(rows, width), received[rows * width :]


def per_device(center, generators, conductivity, cond_table, direction_bank, selection):
    rate_field = lookup_rate(conductivity, cond_table)
    body = jnp.concatenate([center[None], generators], axis=0)
    size = lax.axis_size("slab")
    up = [(i, i + 1) for i in range(size - 1)]
    down = [(j, i) for i, j in up]
    planes = body.shape[1]
    lower = jnp.concatenate([body[:, :2], rate_field[None, :2]], axis=0)
    upper = jnp.concatenate([body[:, planes - 2 :], rate_field[None, planes - 2 :]], axis=0)
    even = lax.axis_index("slab") % 2 == 0
    across = [(i, i + 1) for i in range(1, size - 1, 2)] + [(i, i - 1) for i in range(2, size, 2)]
    within = [(i, i + 1) for i in range(0, size, 2)] + [(i + 1, i) for i in range(0, size, 2)]
    far = lax.ppermute(jnp.where(even, lower, upper), "slab", across)
    near = lax.ppermute(jnp.where(even, upper, lower), "slab", within)
    before = jnp.where(even, far, near)
    after = jnp.where(even, near, far)
    fields = jnp.concatenate([before[:-1], body, after[:-1]], axis=1)
    rate_ext = jnp.concatenate([before[-1, 1:], rate_field, after[-1, :1]], axis=0)
    centre_moved = update(update(fields[:1], rate_ext), rate_field)[0]
    gens_moved = update(update(fields[1:], rate_ext), rate_field)
    fields = jnp.concatenate([centre_moved[None], gens_moved], axis=0)
    radius_local = jnp.sum(jnp.abs(gens_moved), axis=0)
    all_proj = jnp.einsum(
        "bzc,gzc->bg", direction_bank, fields, precision=lax.Precision.HIGHEST
    )
    summed = exchange_sum(all_proj, "slab")
    summed_centre, summed_proj = summed[:, 0], summed[:, 1:]
    partial_value = jnp.sum(jnp.abs(summed_proj), axis=1)
    radius, magnitude = exchange_scatter(radius_local, partial_value, "gen")
    columns = radius.shape[1]
    centre_cols = lax.dynamic_slice_in_dim(
        centre_moved, lax.axis_index("gen") * columns, columns, 1
    )
    hull_lo = centre_cols - radius
    hull_hi = centre_cols + radius
    bank_support = summed_centre + magnitude
    supports = select_rows(selection, bank_support)
    return (hull_lo, hull_hi, supports)


def solution(mesh):
    in_specs = (
        P("slab", None),
        P("gen", "slab", None),
        P("slab", None),
        P(),
        P(None, "slab", None),
        P(),
    )
    out_specs = (P("slab", "gen"), P("slab", "gen"), P())
    return jax.shard_map(
        per_device, mesh=mesh, in_specs=in_specs, out_specs=out_specs, check_vma=False
    )
```

```python
import jax
import jax.numpy as jnp
from jax import lax
from jax.sharding import PartitionSpec as P

NX = 64
NY = 64


TIME_STEP = 0.16


def padded_2(x, sides, width):
    for axis, dim in sides:
        size, length = (lax.axis_size(axis), x.shape[dim])
        up = [(i, (i + 1) % size) for i in range(size - 1)]
        down = [(j, i) for i, j in up]
        last = lax.slice_in_dim(x, length - width, length, axis=dim)
        leading = lax.slice_in_dim(x, 0, width, axis=dim)
        before = lax.ppermute(last, axis, up)
        after = lax.ppermute(leading, axis, down)
        x = jnp.concatenate([before, x, after], axis=dim)
    return x


def lookup_rate(conductivity, cond_table):
    classes = jnp.arange(cond_table.shape[0], dtype=jnp.int32)
    picked = jnp.where(
        conductivity[None] == classes[:, None, None], cond_table[:, None, None], jnp.float32(0.0)
    )
    return TIME_STEP * jnp.sum(picked, axis=0)


def lateral(middle):
    cells = NX * NY
    column = jnp.arange(cells, dtype=jnp.int32) % NY
    widths = [(0, 0)] * (middle.ndim - 1) + [(NY, NY)]
    padded = jnp.pad(middle, widths)
    total = padded[..., 2 * NY :] + padded[..., :cells]
    plus = jnp.where(column < NY - 1, padded[..., NY + 1 : NY + 1 + cells], jnp.float32(0.0))
    minus = jnp.where(column > 0, padded[..., NY - 1 : NY - 1 + cells], jnp.float32(0.0))
    return total + plus + minus


def update(extended, rate_field):
    middle = extended[:, 1:-1]
    zsum = extended[:, 2:] + extended[:, :-2]
    return middle + rate_field * (zsum + lateral(middle) - 6.0 * middle)


def select_rows(selection, values):
    entries = jnp.arange(values.shape[0], dtype=jnp.int32)
    return jnp.sum(
        jnp.where(selection[:, None] == entries[None, :], values[None, :], jnp.float32(0.0)), axis=1
    )


def exchange_sum(x, axis):
    size = lax.axis_size(axis)
    flat = x.reshape(-1)
    copies = jnp.broadcast_to(flat[None], (size, flat.shape[0]))
    received = lax.all_to_all(copies, axis, 0, 0, tiled=True)
    return jnp.sum(received, axis=0).reshape(x.shape)


def exchange_scatter(x, extra, axis):
    size = lax.axis_size(axis)
    rows, cols = x.shape
    width = cols // size
    blocks = x.reshape(rows, size, width)
    padded = jnp.pad(extra, (0, width - extra.shape[0]))
    extras = jnp.broadcast_to(padded[None, None], (1, size, width))
    message = jnp.concatenate([blocks, extras], axis=0)
    received = jnp.sum(lax.all_to_all(message, axis, 1, 1, tiled=True), axis=1)
    return received[:rows], received[rows, : extra.shape[0]]


def per_device(center, generators, conductivity, cond_table, direction_bank, selection):
    rate_field = lookup_rate(conductivity, cond_table)
    body = jnp.concatenate([center[None], generators], axis=0)
    size = lax.axis_size("slab")
    up = [(i, i + 1) for i in range(size - 1)]
    down = [(j, i) for i, j in up]
    planes = body.shape[1]
    lower = jnp.concatenate([body[:, :2], rate_field[None, :2]], axis=0)
    upper = jnp.concatenate([body[:, planes - 2 :], rate_field[None, planes - 2 :]], axis=0)
    even = lax.axis_index("slab") % 2 == 0
    across = [(i, i + 1) for i in range(1, size - 1, 2)] + [(i, i - 1) for i in range(2, size, 2)]
    within = [(i, i + 1) for i in range(0, size, 2)] + [(i + 1, i) for i in range(0, size, 2)]
    far = lax.ppermute(jnp.where(even, lower, upper), "slab", across)
    near = lax.ppermute(jnp.where(even, upper, lower), "slab", within)
    before = jnp.where(even, far, near)
    after = jnp.where(even, near, far)
    fields = jnp.concatenate([before[:-1], body, after[:-1]], axis=1)
    rate_ext = jnp.concatenate([before[-1, 1:], rate_field, after[-1, :1]], axis=0)
    centre_moved = update(update(fields[:1], rate_ext), rate_field)[0]
    gens_moved = update(update(fields[1:], rate_ext), rate_field)
    fields = jnp.concatenate([centre_moved[None], gens_moved], axis=0)
    radius_local = jnp.sum(jnp.abs(gens_moved), axis=0)
    all_proj = jnp.einsum(
        "bzc,gzc->bg", direction_bank, fields, precision=lax.Precision.HIGHEST
    )
    summed = exchange_sum(all_proj, "slab")
    summed_centre, summed_proj = summed[:, 0], summed[:, 1:]
    partial_value = jnp.sum(jnp.abs(summed_proj), axis=1)
    radius, magnitude = exchange_scatter(radius_local, partial_value, "gen")
    columns = radius.shape[1]
    centre_cols = lax.dynamic_slice_in_dim(
        centre_moved, lax.axis_index("gen") * columns, columns, 1
    )
    hull_lo = centre_cols - radius
    hull_hi = centre_cols + radius
    bank_support = summed_centre + magnitude
    supports = select_rows(selection, bank_support)
    return (hull_lo, hull_hi, supports)


def solution(mesh):
    in_specs = (
        P("slab", None),
        P("gen", "slab", None),
        P("slab", None),
        P(),
        P(None, "slab", None),
        P(),
    )
    out_specs = (P("slab", "gen"), P("slab", "gen"), P())
    return jax.shard_map(
        per_device, mesh=mesh, in_specs=in_specs, out_specs=out_specs, check_vma=False
    )
```

```python
import jax
import jax.numpy as jnp
from jax import lax
from jax.sharding import PartitionSpec as P

NX = 64
NY = 64


TIME_STEP = 0.16


def padded_2(x, sides, width):
    for axis, dim in sides:
        size, length = (lax.axis_size(axis), x.shape[dim])
        up = [(i, (i + 1) % size) for i in range(size - 1)]
        down = [(j, i) for i, j in up]
        last = lax.slice_in_dim(x, length - width, length, axis=dim)
        leading = lax.slice_in_dim(x, 0, width, axis=dim)
        before = lax.ppermute(last, axis, up)
        after = lax.ppermute(leading, axis, down)
        x = jnp.concatenate([before, x, after], axis=dim)
    return x


def lookup_rate(conductivity, cond_table):
    classes = jnp.arange(cond_table.shape[0], dtype=jnp.int32)
    picked = jnp.where(
        conductivity[None] == classes[:, None, None], cond_table[:, None, None], jnp.float32(0.0)
    )
    return TIME_STEP * jnp.sum(picked, axis=0)


def lateral(middle):
    cells = NX * NY
    column = jnp.arange(cells, dtype=jnp.int32) % NY
    widths = [(0, 0)] * (middle.ndim - 1) + [(NY, NY)]
    padded = jnp.pad(middle, widths)
    total = padded[..., 2 * NY :] + padded[..., :cells]
    plus = jnp.where(column < NY - 1, padded[..., NY + 1 : NY + 1 + cells], jnp.float32(0.0))
    minus = jnp.where(column > 0, padded[..., NY - 1 : NY - 1 + cells], jnp.float32(0.0))
    return total + plus + minus


def update(extended, rate_field):
    middle = extended[:, 1:-1]
    zsum = extended[:, 2:] + extended[:, :-2]
    return middle + rate_field * (zsum + lateral(middle) - 6.0 * middle)


def select_rows(selection, values):
    entries = jnp.arange(values.shape[0], dtype=jnp.int32)
    return jnp.sum(
        jnp.where(selection[:, None] == entries[None, :], values[None, :], jnp.float32(0.0)), axis=1
    )


def exchange_sum(x, axis):
    size = lax.axis_size(axis)
    flat = x.reshape(-1)
    copies = jnp.broadcast_to(flat[None], (size, flat.shape[0]))
    received = lax.all_to_all(copies, axis, 0, 0, tiled=True)
    return jnp.sum(received, axis=0).reshape(x.shape)


def exchange_scatter(x, extra, axis):
    size = lax.axis_size(axis)
    rows, cols = x.shape
    width = cols // size
    blocks = x.reshape(rows, size, width).transpose(1, 0, 2).reshape(size, rows * width)
    extras = jnp.broadcast_to(extra[None], (size, extra.shape[0]))
    message = jnp.concatenate([blocks, extras], axis=1)
    received = jnp.sum(lax.all_to_all(message, axis, 0, 0, tiled=True), axis=0)
    return received[: rows * width].reshape(rows, width), received[rows * width :]


def per_device(center, generators, conductivity, cond_table, direction_bank, selection):
    rate_field = lookup_rate(conductivity, cond_table)
    body = jnp.concatenate([center[None], generators], axis=0)
    size = lax.axis_size("slab")
    up = [(i, i + 1) for i in range(size - 1)]
    down = [(j, i) for i, j in up]
    planes = body.shape[1]
    lower = jnp.concatenate([body[:, :2], rate_field[None, :2]], axis=0)
    upper = jnp.concatenate([body[:, planes - 2 :], rate_field[None, planes - 2 :]], axis=0)
    even = lax.axis_index("slab") % 2 == 0
    across = [(i, i + 1) for i in range(1, size - 1, 2)] + [(i, i - 1) for i in range(2, size, 2)]
    within = [(i, i + 1) for i in range(0, size, 2)] + [(i + 1, i) for i in range(0, size, 2)]
    far = lax.ppermute(jnp.where(even, lower, upper), "slab", across)
    inner, far = lax.optimization_barrier((jnp.where(even, upper, lower), far))
    near = lax.ppermute(inner, "slab", within)
    before = jnp.where(even, far, near)
    after = jnp.where(even, near, far)
    fields = jnp.concatenate([before[:-1], body, after[:-1]], axis=1)
    rate_ext = jnp.concatenate([before[-1, 1:], rate_field, after[-1, :1]], axis=0)
    centre_moved = update(update(fields[:1], rate_ext), rate_field)[0]
    gens_moved = update(update(fields[1:], rate_ext), rate_field)
    fields = jnp.concatenate([centre_moved[None], gens_moved], axis=0)
    radius_local = jnp.sum(jnp.abs(gens_moved), axis=0)
    all_proj = jnp.einsum(
        "bzc,gzc->bg", direction_bank, fields, precision=lax.Precision.HIGHEST
    )
    summed = exchange_sum(all_proj, "slab")
    summed_centre, summed_proj = summed[:, 0], summed[:, 1:]
    partial_value = jnp.sum(jnp.abs(summed_proj), axis=1)
    radius, magnitude = exchange_scatter(radius_local, partial_value, "gen")
    columns = radius.shape[1]
    centre_cols = lax.dynamic_slice_in_dim(
        centre_moved, lax.axis_index("gen") * columns, columns, 1
    )
    hull_lo = centre_cols - radius
    hull_hi = centre_cols + radius
    bank_support = summed_centre + magnitude
    supports = select_rows(selection, bank_support)
    return (hull_lo, hull_hi, supports)


def solution(mesh):
    in_specs = (
        P("slab", None),
        P("gen", "slab", None),
        P("slab", None),
        P(),
        P(None, "slab", None),
        P(),
    )
    out_specs = (P("slab", "gen"), P("slab", "gen"), P())
    return jax.shard_map(
        per_device, mesh=mesh, in_specs=in_specs, out_specs=out_specs, check_vma=False
    )
```
